512 devices in a mesh: dp: 8 (over z), expert: 64 (over y, x, core).
Axes of the slice: x: 4, y: 8, z: 8, core: 2. Of those that a mesh axis runs over, the one named last changes fastest.
Arguments:
- query: bfloat16 [128, 8192], P('dp'), may hold values from -1200 to 1200
- new_kv: bfloat16 [128, 1024], P('dp'), may hold values from -5 to 5
- kv_cache: bfloat16 [128, 1024, 1024], P('dp', 'expert'), may hold values from -6 to 6
- lengths: int32 [128], P('dp'), may hold values from 2 to 1024, as said below
- fork_parent: int32 [64], replicated, may hold values from 0 to 127, as said below
- fork_child: int32 [64], replicated, may hold values from 0 to 126, as said below
- fork_block: int32 [64], replicated, may hold values from 0 to 63, as said below
- out_weight: bfloat16 [8192, 4096], P('expert'), may hold values from -1 to 1
- residual: bfloat16 [128, 4096], P('dp'), may hold values from -300 to 300
- route_ids: int32 [128, 8], replicated, may hold values from 0 to 63, all different within a row; in each aligned block of 16 rows (0 to 15, 16 to 31, ...) at most 4 rows name the same one
- route_weights: float32 [128, 8], replicated, may hold values from 0.02 to 0.3
- w_gate: bfloat16 [64, 4096, 1024], P('expert', None, 'dp'), may hold values from -0.09375 to 0.09375
- w_up: bfloat16 [64, 4096, 1024], P('expert', None, 'dp'), may hold values from -0.09375 to 0.09375
- w_down: bfloat16 [64, 1024, 4096], P('expert', 'dp'), may hold values from -0.1875 to 0.1875
Outputs:
- attn_proj: bfloat16 [128, 4096], P('dp', 'expert')
- expert_mix: bfloat16 [128, 4096], P('dp', 'expert')
The draws below stay inside these ranges and needn't reach their ends.
Inputs may be any that keep to these rules, and one draw needn't show every extreme that they name: `lengths`: at least 2; a fork's child has its parent's length. `fork_parent`: fork g * 8 + d takes its parent from the branches g * 16 to (g + 1) * 16 - 1 and its child from d * 16 to (d + 1) * 16 - 1; parents are distinct, children are distinct, and no child is a parent. `fork_child`: see fork_parent. `fork_block`: at most the block that holds the parent's last cached position, (lengths - 1) // 16. `route_ids`: in each aligned block of 16 rows no expert is named by more than 4 rows, a bound that some block reaches.
All inputs are finite; a program needn't handle non-finite values.
Results may differ from the reference program's by a relative error of at most 0.024.
Values may be sent and summed in bfloat16 or wider, within the bound.
No kernel may reach another device: no remote copies, remote signals or barrier semaphores. Data moves between devices by JAX's collectives and lax.ppermute only.
A program may use at most 128 MiB of HBM per device.

```python
import math
import jax
import jax.numpy as jnp
import numpy as np
from jax import lax

D = 4096
HD = 128
KVH = 4
HEADS = 64
EXPERTS = 64
FF = 1024
TOP = 8
BR_GRP = 16
CTX_DEV = 16
B = 128
CTX = 1024
KVW = 1024
QW = 8192
CAP = 4
FORKS = 64


def swap_into(row, value, place):
    where_now = jnp.sum(jnp.where(row == value, jnp.arange(row.shape[0], dtype=jnp.int32), 0)).astype(jnp.int32)
    held = row[place]
    return row.at[where_now].set(held).at[place].set(value)


def fork_plan(key):
    plan_key = jax.random.fold_in(key, 11)
    groups = B // BR_GRP

    def shuffle(subkey):
        return jax.random.permutation(subkey, BR_GRP)
    orders = jax.vmap(shuffle)(jax.random.split(plan_key, groups)).astype(jnp.int32)
    last_row = swap_into(orders[groups - 1], BR_GRP - 1, 0)
    last_row = swap_into(last_row, BR_GRP - 2, groups)
    orders = orders.at[groups - 1].set(last_row.astype(jnp.int32))
    group_start = jnp.arange(groups, dtype=jnp.int32) * BR_GRP
    parent = (group_start[:, None] + orders[:, :groups]).reshape(-1).astype(jnp.int32)
    child = (group_start[None, :] + orders[:, groups:2 * groups].T).reshape(-1).astype(jnp.int32)
    drawn = jax.random.randint(jax.random.fold_in(plan_key, 1), (B,), 2, CTX + 1, jnp.int32)
    drawn = drawn.at[parent[0]].set(CTX)
    lengths = drawn.at[child].set(drawn[parent])
    last_block = (lengths[parent] - 1) // CTX_DEV
    fork_at = jax.random.randint(jax.random.fold_in(plan_key, 2), (FORKS,), 0, 1 << 20, jnp.int32) % (last_block + 1)
    fork_at = fork_at.at[0].set(last_block[0])
    return (lengths.astype(jnp.int32), parent, child, fork_at.astype(jnp.int32))


def draw_lengths(key, part):
    return fork_plan(key)[0]


def draw_fork_parent(key, part):
    return fork_plan(key)[1]


def draw_fork_child(key, part):
    return fork_plan(key)[2]


def draw_fork_block(key, part):
    return fork_plan(key)[3]


def first_keys(key):
    return jnp.clip(jax.random.normal(jax.random.fold_in(key, 23), (B, KVH * HD), jnp.float32), -4.0, 4.0)


def draw_kv_cache(key, part):
    shape = (B, CTX, KVW)
    cache = jnp.clip(jax.random.normal(jax.random.fold_in(key, 5), shape, jnp.float32), -6.0, 6.0)
    leading = first_keys(key)
    cache = cache.at[:, 0, :KVH * HD].set(leading)
    return cache.astype(jnp.bfloat16)


def draw_query(key, part):
    shape = (B, QW)
    entries = jnp.clip(jax.random.normal(jax.random.fold_in(key, 3), shape, jnp.float32), -6.0, 6.0)
    return entries.astype(jnp.bfloat16)


def draw_residual(key, part):
    shape = (B, D)
    row_scale = 10.0 ** jax.random.uniform(jax.random.fold_in(key, 9), (B, 1), jnp.float32, 0.0, 0.6)
    column_pos = jnp.arange(D, dtype=jnp.float32)[None, :] / D
    base_values = jnp.clip(jax.random.normal(jax.random.fold_in(key, 8), shape, jnp.float32), -5.0, 5.0)
    column_scale = 10.0 ** column_pos
    return (base_values * row_scale * column_scale).astype(jnp.bfloat16)


def levels(key, dims, cuts, smallest, largest):
    gain = 1.0
    for axis_at, parts in cuts:
        heights = jax.random.uniform(jax.random.fold_in(jax.random.fold_in(key, 6), axis_at), (parts,), jnp.float32, smallest / len(cuts), largest / len(cuts))
        gain = gain * jnp.repeat(jnp.exp(heights), dims[axis_at] // parts).reshape((-1,) + (1,) * (len(dims) - 1 - axis_at))
    return gain


def shared_out(rng, own, number, rows, number_of, top, limit, lean):
    ranking = jax.random.permutation(rng, number_of)
    heavy_load, ordinary = shares(number_of, rows * top, limit, lean, True), shares(number_of, rows * top, limit, lean, False)
    places = jnp.arange(number_of)

    def named(sizes, rotation):
        used = int((sizes > 0).sum())
        fixed = max(1, used // 4)
        moved = fixed + (places - fixed + rotation * (used - fixed)) % max(1, number_of - fixed)
        return jnp.zeros((number_of,), jnp.int32).at[ranking[jnp.where(places < fixed, places, moved)]].set(jnp.asarray(sizes, jnp.int32))

    sizes = jnp.where(number % 4 == 0, named(heavy_load, number // 4), named(ordinary, number - number // 4 - 1))
    mixed = jax.random.permutation(jax.random.fold_in(own, 3), number_of)
    source_of, sink = mixed[0:number_of // 2 * 2:2], mixed[1:number_of // 2 * 2:2]
    slack = jnp.minimum(sizes[source_of] - 1, limit - sizes[sink]) // 2
    slack = jnp.where((source_of == ranking[0]) | (sink == ranking[0]) | (sizes[sink] == 0), 0, jnp.maximum(slack, 0))
    moved = jax.random.randint(jax.random.fold_in(own, 4), (number_of // 2,), 0, 1 << 20) % (slack + 1)
    sizes = sizes.at[source_of].add(-moved).at[sink].add(moved)
    labels = jnp.searchsorted(jnp.cumsum(sizes), jnp.arange(rows * top), side="right").astype(jnp.int32)
    table = labels.reshape(top, rows).T
    table = table[jax.random.permutation(jax.random.fold_in(own, 1), rows)]
    rotation = jax.random.randint(jax.random.fold_in(own, 2), (rows, 1), 0, top)
    return jnp.take_along_axis(table, (jnp.arange(top)[None, :] + rotation) % top, axis=1)


def shares(count, total, reach, skew, full):
    weights = [(1 << 20) // math.isqrt(grade ** skew) + 1 for grade in range(1, count + 1)]
    largest = reach if full else min(reach, max(-(-total // count), total * weights[0] // sum(weights)))
    least = 1 if total - largest >= count - 1 else 0
    counts, spare = [largest] + [least] * (count - 1), total - largest - least * (count - 1)
    while spare > 0:
        candidates = [i for i in range(1, count) if counts[i] < largest] or [i for i in range(1, count) if counts[i] < reach]
        whole, left = sum([weights[i] for i in candidates]), spare
        for i in candidates:
            more = min(reach - counts[i], max(1, left * weights[i] // whole), spare)
            counts[i] = counts[i] + more
            spare = spare - more
    return np.array(counts)


def bell_draw(rng, shape, spread, reach, pieces=(), held_as=jnp.bfloat16):
    array = jax.random.normal(rng, shape, jnp.float32) * spread
    if len(pieces) > 0:
        array = levels(rng, shape, pieces, -0.22, 0.18) * array
    return jnp.clip(array, min=-reach, max=reach).astype(held_as)


def setup_inputs(seed: int = 0) -> dict:
    seeds = jax.random.split(jax.random.key(seed), 15)
    query = draw_query(jax.random.fold_in(seeds[14], 71), 0)
    new_kv = bell_draw(seeds[1], (B, KVW), 1.0, 5.0, ((0, 8),))
    kv_cache = draw_kv_cache(jax.random.fold_in(seeds[14], 71), 0)
    lengths = draw_lengths(jax.random.fold_in(seeds[14], 71), 0)
    fork_parent = draw_fork_parent(jax.random.fold_in(seeds[14], 71), 0)
    fork_child = draw_fork_child(jax.random.fold_in(seeds[14], 71), 0)
    fork_block = draw_fork_block(jax.random.fold_in(seeds[14], 71), 0)
    out_weight = bell_draw(seeds[7], (QW, D), (HD // 4) ** -0.5, 1.0, ((0, 64),))
    residual = draw_residual(jax.random.fold_in(seeds[14], 71), 0)
    route_ids_keys = jax.random.split(jax.random.fold_in(seeds[9], 1), B // BR_GRP)
    route_ids_turns = jax.random.permutation(jax.random.fold_in(seeds[9], 3), B // BR_GRP)
    route_ids = jax.vmap(lambda own, number: shared_out(jax.random.fold_in(seeds[9], 2), own, number, BR_GRP, EXPERTS, TOP, CAP, 2))(route_ids_keys, route_ids_turns).reshape((B, TOP))
    route_weights = jnp.clip(jnp.exp(jax.random.uniform(seeds[10], (B, TOP), jnp.float32, math.log(0.02), math.log(0.3))), 0.02, 0.3)
    w_gate = bell_draw(seeds[11], (EXPERTS, D, FF), D ** -0.5, 0.09375, ((0, 64), (2, 8)))
    w_up = bell_draw(seeds[12], (EXPERTS, D, FF), D ** -0.5, 0.09375, ((0, 64), (2, 8)))
    w_down = bell_draw(seeds[13], (EXPERTS, FF, D), FF ** -0.5, 0.1875, ((0, 64), (1, 8)))
    return {"query": query, "new_kv": new_kv, "kv_cache": kv_cache, "lengths": lengths, "fork_parent": fork_parent, "fork_child": fork_child, "fork_block": fork_block, "out_weight": out_weight, "residual": residual, "route_ids": route_ids, "route_weights": route_weights, "w_gate": w_gate, "w_up": w_up, "w_down": w_down}


def attend_branch(row_items):
    query_row, new_row, cache_rows, length = row_items
    grouping = HEADS // KVH
    key_width = KVH * HD
    score_scale = 1.0 / math.sqrt(HD)
    grouped = query_row.astype(jnp.float32).reshape(KVH, grouping, HD)
    cached_keys = cache_rows[:, :key_width].astype(jnp.float32).reshape(CTX, KVH, HD)
    cached_values = cache_rows[:, key_width:].astype(jnp.float32).reshape(CTX, KVH, HD)
    new_key = new_row[:key_width].astype(jnp.float32).reshape(KVH, HD)
    new_value = new_row[key_width:].astype(jnp.float32).reshape(KVH, HD)
    scores = jnp.einsum('kgd,pkd->kgp', grouped, cached_keys) * score_scale
    own_score = jnp.einsum('kgd,kd->kg', grouped, new_key) * score_scale
    visible = jnp.arange(CTX, dtype=jnp.int32) < length
    scores = jnp.where(visible[None, None, :], scores, -jnp.inf)
    highest = jnp.maximum(lax.optimization_barrier(jnp.max(scores, axis=-1)), own_score)
    weights = jnp.exp(scores - highest[..., None])
    own_weight = jnp.exp(own_score - highest)
    weight_sum = lax.optimization_barrier(jnp.sum(weights, axis=-1)) + own_weight
    rounded = lax.optimization_barrier(weights.astype(jnp.bfloat16)).astype(jnp.float32)
    own_rounded = lax.optimization_barrier(own_weight.astype(jnp.bfloat16)).astype(jnp.float32)
    gathered = jnp.einsum('kgp,pkd->kgd', rounded, cached_values)
    gathered = gathered + own_rounded[..., None] * new_value[:, None, :]
    return (gathered / weight_sum[..., None]).reshape(-1).astype(jnp.bfloat16)

def reference(query, new_kv, kv_cache, lengths, fork_parent, fork_child, fork_block, out_weight, residual, route_ids, route_weights, w_gate, w_up, w_down):
    positions = jnp.arange(CTX, dtype=jnp.int32)
    starts = fork_block * CTX_DEV
    beyond = positions[None, :] >= starts[:, None]
    copied = jnp.where(beyond[:, :, None], kv_cache[fork_parent], kv_cache[fork_child])
    forked_cache = kv_cache.at[fork_child].set(copied)
    heads_out = lax.map(attend_branch, (query, new_kv, forked_cache, lengths))
    projected = jnp.dot(heads_out, out_weight, preferred_element_type=jnp.float32)
    attn_proj = projected.astype(jnp.bfloat16)
    stream = residual.astype(jnp.float32) + projected
    normed = (stream * lax.rsqrt(lax.optimization_barrier(jnp.mean(stream * stream, axis=1, keepdims=True)) + 1e-06)).astype(jnp.bfloat16)

    def expert_token(token_items):
        token_row, expert_ids, gate_values = token_items
        gate_mats = w_gate[expert_ids].astype(jnp.float32)
        up_mats = w_up[expert_ids].astype(jnp.float32)
        down_mats = w_down[expert_ids].astype(jnp.float32)
        row_wide = token_row.astype(jnp.float32)
        gate_proj = jnp.einsum('d,kdf->kf', row_wide, gate_mats)
        up_proj = jnp.einsum('d,kdf->kf', row_wide, up_mats)
        hidden = (jax.nn.silu(gate_proj) * up_proj).astype(jnp.bfloat16)
        expert_out = jnp.einsum('kf,kfd->kd', hidden.astype(jnp.float32), down_mats)
        return lax.optimization_barrier(jnp.sum(gate_values[:, None] * expert_out, axis=0)).astype(jnp.bfloat16)
    expert_mix = lax.map(expert_token, (normed, route_ids, route_weights))
    return (attn_proj, expert_mix)
```

```python
import math

import jax
import jax.numpy as jnp
from jax import lax
from jax.sharding import PartitionSpec as P

HD = 128
KVH = 4


def spread_to_owners(blocks, axis):
    return lax.all_to_all(blocks, axis, 0, 0, tiled=True)


def gather_from_all(block, axis):
    count = lax.axis_size(axis)
    stacked = jnp.broadcast_to(block[None], (count,) + block.shape)
    return spread_to_owners(stacked, axis)


def shards(
    query,
    new_kv,
    kv_cache,
    lengths,
    fork_parent,
    fork_child,
    fork_block,
    out_weight,
    residual,
    route_ids,
    route_weights,
    w_gate,
    w_up,
    w_down,
):
    groups = lax.axis_size("dp")
    owners = lax.axis_size("expert")
    group_index = lax.axis_index("dp")
    owner_index = lax.axis_index("expert")
    local_rows = query.shape[0]
    positions_dev = kv_cache.shape[1]
    key_width = KVH * HD
    head_count = query.shape[1] // HD
    grouping = head_count // KVH
    own_heads = head_count // owners
    model_width = residual.shape[1]
    columns = model_width // owners

    outgoing = (
        lax.dynamic_slice_in_dim(fork_parent, group_index * groups, groups)
        - group_index * local_rows
    )
    out_blocks = lax.dynamic_slice_in_dim(fork_block, group_index * groups, groups)
    send_rows = jnp.where(
        (owner_index >= out_blocks)[:, None, None],
        kv_cache[outgoing],
        jnp.zeros((), kv_cache.dtype),
    )
    arrived = lax.all_to_all(send_rows, "dp", split_axis=0, concat_axis=0, tiled=True)
    incoming = jnp.arange(groups, dtype=jnp.int32) * groups + group_index
    targets = fork_child[incoming] - group_index * local_rows
    take_new = owner_index >= fork_block[incoming]
    cache = kv_cache.at[targets].set(jnp.where(take_new[:, None, None], arrived, kv_cache[targets]))

    score_scale = 1.0 / math.sqrt(HD)
    positions = owner_index * positions_dev + jnp.arange(positions_dev, dtype=jnp.int32)
    visible = positions[None, :] < lengths[:, None]
    cached_keys = cache[:, :, :key_width].reshape(local_rows, positions_dev, KVH, HD)
    cached_values = cache[:, :, key_width:].reshape(local_rows, positions_dev, KVH, HD)
    grouped = query.reshape(local_rows, KVH, grouping, HD)
    scores = (
        jnp.einsum("bkgd,bpkd->bkgp", grouped, cached_keys, preferred_element_type=jnp.float32)
        * score_scale
    )
    scores = jnp.where(visible[:, None, None, :], scores, -1e30)
    highest = jnp.max(scores, axis=3)
    weights = jnp.where(visible[:, None, None, :], jnp.exp(scores - highest[..., None]), 0.0)
    weight_sum = jnp.sum(weights, axis=3)
    partial_out = jnp.einsum(
        "bkgp,bpkd->bkgd",
        weights.astype(jnp.bfloat16),
        cached_values,
        preferred_element_type=jnp.float32,
    )

    send_out = partial_out.reshape(local_rows, owners, own_heads, HD).transpose(1, 0, 2, 3)
    send_peak = highest.reshape(local_rows, owners, own_heads).transpose(1, 0, 2)
    send_sum = weight_sum.reshape(local_rows, owners, own_heads).transpose(1, 0, 2)
    got_out = spread_to_owners(send_out.astype(jnp.bfloat16), "expert").astype(jnp.float32)
    got_peak = spread_to_owners(send_peak, "expert")
    got_sum = spread_to_owners(send_sum, "expert")
    head_peak = jnp.max(got_peak, axis=0)
    factors = jnp.exp(got_peak - head_peak[None])
    head_out = jnp.sum(got_out * factors[..., None], axis=0)
    head_sum = jnp.sum(got_sum * factors, axis=0)

    own_query = lax.dynamic_slice_in_dim(query, owner_index * own_heads * HD, own_heads * HD, 1)
    own_query = own_query.reshape(local_rows, own_heads, HD).astype(jnp.float32)
    kv_index = (owner_index * own_heads + jnp.arange(own_heads, dtype=jnp.int32)) // grouping
    new_keys = jnp.take(
        new_kv[:, :key_width].reshape(local_rows, KVH, HD), kv_index, axis=1
    ).astype(jnp.float32)
    new_values = jnp.take(
        new_kv[:, key_width:].reshape(local_rows, KVH, HD), kv_index, axis=1
    ).astype(jnp.float32)
    own_score = jnp.sum(own_query * new_keys, axis=2) * score_scale
    new_peak = jnp.maximum(head_peak, own_score)
    old_factor = jnp.exp(head_peak - new_peak)
    own_weight = jnp.exp(own_score - new_peak)
    denominator = head_sum * old_factor + own_weight
    own_rounded = lax.optimization_barrier(own_weight.astype(jnp.bfloat16)).astype(jnp.float32)
    attended = (
        head_out * old_factor[..., None] + own_rounded[..., None] * new_values
    ) / denominator[..., None]
    attended = attended.astype(jnp.bfloat16).reshape(local_rows, own_heads * HD)

    proj_terms = jnp.dot(attended, out_weight, preferred_element_type=jnp.float32)
    proj_blocks = proj_terms.reshape(local_rows, owners, columns).transpose(1, 0, 2)
    projected_cols = jnp.sum(spread_to_owners(proj_blocks, "expert"), axis=0)
    attn_cols = projected_cols.astype(jnp.bfloat16)
    residual_cols = lax.dynamic_slice_in_dim(residual, owner_index * columns, columns, 1)
    stream_cols = residual_cols.astype(jnp.float32) + projected_cols
    stream = gather_from_all(stream_cols, "expert").transpose(1, 0, 2).reshape(
        local_rows, model_width
    )
    inverse = lax.rsqrt(jnp.sum(stream * stream, axis=1, keepdims=True) / model_width + 1e-06)
    normed = (stream * inverse).astype(jnp.bfloat16)

    top_k = route_ids.shape[1]
    experts_total = w_gate.shape[0] * owners
    capacity = max(2, 2 * local_rows * top_k // experts_total)
    own_ids = lax.dynamic_slice_in_dim(route_ids, group_index * local_rows, local_rows, 0)
    own_gates = lax.dynamic_slice_in_dim(route_weights, group_index * local_rows, local_rows, 0)
    expert_ids = jnp.arange(experts_total, dtype=jnp.int32)
    matched = (own_ids[:, :, None] == expert_ids[None, None, :]).astype(jnp.int32)
    flat_matched = matched.reshape(local_rows * top_k, experts_total)
    ranking = jnp.cumsum(flat_matched, axis=0) - 1
    slot_ids = jnp.arange(capacity, dtype=jnp.int32)
    hit = (flat_matched[:, :, None] == 1) & (ranking[:, :, None] == slot_ids[None, None, :])
    hit = hit.astype(jnp.float32).reshape(local_rows, top_k, experts_total, capacity)
    slot_weight = jnp.sum(hit * own_gates[:, :, None, None], axis=1)
    own_hit = lax.dynamic_index_in_dim(hit, owner_index, 2, False)
    dispatch = jnp.sum(own_hit, axis=1).T
    routed = jnp.dot(
        dispatch.astype(jnp.bfloat16), normed, preferred_element_type=jnp.float32
    ).astype(jnp.bfloat16)
    piece = gather_from_all(routed, "dp").reshape(groups * capacity, model_width)
    gate_proj = jnp.dot(piece, w_gate[0], preferred_element_type=jnp.float32)
    up_proj = jnp.dot(piece, w_up[0], preferred_element_type=jnp.float32)
    hidden = (jax.nn.silu(gate_proj) * up_proj).astype(jnp.bfloat16)
    outputs = jnp.dot(hidden, w_down[0], preferred_element_type=jnp.float32)
    partials = spread_to_owners(
        outputs.astype(jnp.bfloat16).reshape(groups, capacity, model_width), "dp"
    )
    summed = jnp.sum(partials.astype(jnp.float32), axis=0)
    slot_blocks = summed.reshape(capacity, owners, columns).transpose(1, 0, 2)
    got_slots = spread_to_owners(slot_blocks, "expert")
    mix_cols = jnp.einsum(
        "tes,esc->tc", slot_weight, got_slots, precision=lax.Precision.HIGHEST
    ).astype(jnp.bfloat16)
    return (attn_cols, mix_cols)


def solution(mesh):
    in_specs = (
        P("dp", None),
        P("dp", None),
        P("dp", "expert", None),
        P("dp"),
        P(),
        P(),
        P(),
        P("expert", None),
        P("dp", None),
        P(),
        P(),
        P("expert", None, "dp"),
        P("expert", None, "dp"),
        P("expert", "dp", None),
    )
    out_specs = (P("dp", "expert"), P("dp", "expert"))
    return jax.shard_map(shards, mesh=mesh, in_specs=in_specs, out_specs=out_specs, check_vma=False)
```

```python
import math

import jax
import jax.numpy as jnp
from jax import lax
from jax.sharding import PartitionSpec as P

HD = 128
KVH = 4


def spread_to_owners(blocks, axis):
    return lax.all_to_all(blocks, axis, 0, 0, tiled=True)


def shards(
    query,
    new_kv,
    kv_cache,
    lengths,
    fork_parent,
    fork_child,
    fork_block,
    out_weight,
    residual,
    route_ids,
    route_weights,
    w_gate,
    w_up,
    w_down,
):
    groups = lax.axis_size("dp")
    owners = lax.axis_size("expert")
    group_index = lax.axis_index("dp")
    owner_index = lax.axis_index("expert")
    local_rows = query.shape[0]
    positions_dev = kv_cache.shape[1]
    key_width = KVH * HD
    head_count = query.shape[1] // HD
    grouping = head_count // KVH
    own_heads = head_count // owners
    model_width = residual.shape[1]
    columns = model_width // owners

    outgoing = (
        lax.dynamic_slice_in_dim(fork_parent, group_index * groups, groups)
        - group_index * local_rows
    )
    out_blocks = lax.dynamic_slice_in_dim(fork_block, group_index * groups, groups)
    send_rows = jnp.where(
        (owner_index >= out_blocks)[:, None, None],
        kv_cache[outgoing],
        jnp.zeros((), kv_cache.dtype),
    )
    arrived = lax.all_to_all(send_rows, "dp", split_axis=0, concat_axis=0, tiled=True)
    incoming = jnp.arange(groups, dtype=jnp.int32) * groups + group_index
    targets = fork_child[incoming] - group_index * local_rows
    take_new = owner_index >= fork_block[incoming]
    cache = kv_cache.at[targets].set(jnp.where(take_new[:, None, None], arrived, kv_cache[targets]))

    score_scale = 1.0 / math.sqrt(HD)
    positions = owner_index * positions_dev + jnp.arange(positions_dev, dtype=jnp.int32)
    visible = positions[None, :] < lengths[:, None]
    cached_keys = cache[:, :, :key_width].reshape(local_rows, positions_dev, KVH, HD)
    cached_values = cache[:, :, key_width:].reshape(local_rows, positions_dev, KVH, HD)
    grouped = query.reshape(local_rows, KVH, grouping, HD)
    scores = (
        jnp.einsum("bkgd,bpkd->bkgp", grouped, cached_keys, preferred_element_type=jnp.float32)
        * score_scale
    )
    scores = jnp.where(visible[:, None, None, :], scores, -1e30)
    highest = jnp.max(scores, axis=3)
    weights = jnp.where(visible[:, None, None, :], jnp.exp(scores - highest[..., None]), 0.0)
    weight_sum = jnp.sum(weights, axis=3)
    partial_out = jnp.einsum(
        "bkgp,bpkd->bkgd",
        weights.astype(jnp.bfloat16),
        cached_values,
        preferred_element_type=jnp.float32,
    )

    head_block = local_rows * own_heads
    send_out = partial_out.reshape(local_rows, owners, own_heads, HD).transpose(1, 0, 2, 3)
    send_peak = highest.reshape(local_rows, owners, own_heads).transpose(1, 0, 2)
    send_sum = weight_sum.reshape(local_rows, owners, own_heads).transpose(1, 0, 2)
    packed = jnp.concatenate(
        [
            send_out.reshape(owners, head_block * HD),
            send_peak.reshape(owners, head_block),
            send_sum.reshape(owners, head_block),
        ],
        axis=1,
    )
    got = spread_to_owners(packed, "expert")
    got_out = got[:, : head_block * HD].reshape(owners, local_rows, own_heads, HD)
    got_peak = got[:, head_block * HD : head_block * (HD + 1)].reshape(owners, local_rows, own_heads)
    got_sum = got[:, head_block * (HD + 1) :].reshape(owners, local_rows, own_heads)
    head_peak = jnp.max(got_peak, axis=0)
    factors = jnp.exp(got_peak - head_peak[None])
    head_out = jnp.sum(got_out * factors[..., None], axis=0)
    head_sum = jnp.sum(got_sum * factors, axis=0)

    own_query = lax.dynamic_slice_in_dim(query, owner_index * own_heads * HD, own_heads * HD, 1)
    own_query = own_query.reshape(local_rows, own_heads, HD).astype(jnp.float32)
    kv_index = (owner_index * own_heads + jnp.arange(own_heads, dtype=jnp.int32)) // grouping
    new_keys = jnp.take(
        new_kv[:, :key_width].reshape(local_rows, KVH, HD), kv_index, axis=1
    ).astype(jnp.float32)
    new_values = jnp.take(
        new_kv[:, key_width:].reshape(local_rows, KVH, HD), kv_index, axis=1
    ).astype(jnp.float32)
    own_score = jnp.sum(own_query * new_keys, axis=2) * score_scale
    new_peak = jnp.maximum(head_peak, own_score)
    old_factor = jnp.exp(head_peak - new_peak)
    own_weight = jnp.exp(own_score - new_peak)
    denominator = head_sum * old_factor + own_weight
    own_rounded = lax.optimization_barrier(own_weight.astype(jnp.bfloat16)).astype(jnp.float32)
    attended = (
        head_out * old_factor[..., None] + own_rounded[..., None] * new_values
    ) / denominator[..., None]
    attended = attended.astype(jnp.bfloat16).reshape(local_rows, own_heads * HD)

    proj_terms = jnp.dot(attended, out_weight, preferred_element_type=jnp.float32)
    proj_blocks = proj_terms.reshape(local_rows, owners, columns).transpose(1, 0, 2)
    projected_cols = jnp.sum(spread_to_owners(proj_blocks, "expert"), axis=0)
    attn_cols = projected_cols.astype(jnp.bfloat16)
    residual_cols = lax.dynamic_slice_in_dim(residual, owner_index * columns, columns, 1)
    stream_cols = residual_cols.astype(jnp.float32) + projected_cols

    top_k = route_ids.shape[1]
    experts_total = w_gate.shape[0] * owners
    capacity = max(2, 2 * local_rows * top_k // experts_total)
    own_ids = lax.dynamic_slice_in_dim(route_ids, group_index * local_rows, local_rows, 0)
    own_gates = lax.dynamic_slice_in_dim(route_weights, group_index * local_rows, local_rows, 0)
    expert_ids = jnp.arange(experts_total, dtype=jnp.int32)
    matched = (own_ids[:, :, None] == expert_ids[None, None, :]).astype(jnp.int32)
    flat_matched = matched.reshape(local_rows * top_k, experts_total)
    ranking = jnp.cumsum(flat_matched, axis=0) - 1
    slot_ids = jnp.arange(capacity, dtype=jnp.int32)
    hit = (flat_matched[:, :, None] == 1) & (ranking[:, :, None] == slot_ids[None, None, :])
    hit = hit.astype(jnp.int32).reshape(local_rows, top_k, experts_total, capacity)
    slot_weight = jnp.sum(hit.astype(jnp.float32) * own_gates[:, :, None, None], axis=1)
    slot_token = jnp.sum(hit, axis=1)
    token_ids = jnp.arange(local_rows, dtype=jnp.int32)
    slot_source = jnp.sum(slot_token * token_ids[:, None, None], axis=0)
    slot_used = jnp.sum(slot_token, axis=0) > 0

    slot_cols = jnp.where(slot_used[:, :, None], stream_cols[slot_source], 0.0)
    slot_cols = jnp.broadcast_to(slot_cols[None], (groups,) + slot_cols.shape)
    slot_cols = slot_cols.reshape(groups * experts_total, capacity, columns)
    rows_in = spread_to_owners(slot_cols, ("dp", "expert"))
    rows_in = rows_in.reshape(groups, owners, capacity, columns).transpose(0, 2, 1, 3)
    stream_rows = rows_in.reshape(groups * capacity, model_width)
    inverse = lax.rsqrt(
        jnp.sum(stream_rows * stream_rows, axis=1, keepdims=True) / model_width + 1e-06
    )
    piece = (stream_rows * inverse).astype(jnp.bfloat16)
    gate_proj = jnp.dot(piece, w_gate[0], preferred_element_type=jnp.float32)
    up_proj = jnp.dot(piece, w_up[0], preferred_element_type=jnp.float32)
    hidden = (jax.nn.silu(gate_proj) * up_proj).astype(jnp.bfloat16)
    outputs = jnp.dot(hidden, w_down[0], preferred_element_type=jnp.float32)

    out_blocks = outputs.astype(jnp.bfloat16).reshape(groups, capacity, owners, columns)
    out_blocks = out_blocks.transpose(0, 2, 1, 3).reshape(groups * owners, capacity, columns)
    partials = spread_to_owners(out_blocks, ("dp", "expert"))
    partials = partials.reshape(groups, experts_total, capacity, columns)
    summed = jnp.sum(partials.astype(jnp.float32), axis=0)
    mix_cols = jnp.einsum(
        "tes,esc->tc", slot_weight, summed, precision=lax.Precision.HIGHEST
    ).astype(jnp.bfloat16)
    return (attn_cols, mix_cols)


def solution(mesh):
    in_specs = (
        P("dp", None),
        P("dp", None),
        P("dp", "expert", None),
        P("dp"),
        P(),
        P(),
        P(),
        P("expert", None),
        P("dp", None),
        P(),
        P(),
        P("expert", None, "dp"),
        P("expert", None, "dp"),
        P("expert", "dp", None),
    )
    out_specs = (P("dp", "expert"), P("dp", "expert"))
    return jax.shard_map(shards, mesh=mesh, in_specs=in_specs, out_specs=out_specs, check_vma=False)
```

```python
import math

import jax
import jax.numpy as jnp
from jax import lax
from jax.sharding import PartitionSpec as P

HD = 128
KVH = 4


def spread_to_owners(blocks, axis):
    return lax.all_to_all(blocks, axis, 0, 0, tiled=True)


def split_three(values):
    high = lax.reduce_precision(values, exponent_bits=8, mantissa_bits=7)
    rest = values - high
    middle = lax.reduce_precision(rest, exponent_bits=8, mantissa_bits=7)
    low = rest - middle
    return jnp.stack([high, middle, low]).astype(jnp.bfloat16)


def shards(
    query,
    new_kv,
    kv_cache,
    lengths,
    fork_parent,
    fork_child,
    fork_block,
    out_weight,
    residual,
    route_ids,
    route_weights,
    w_gate,
    w_up,
    w_down,
):
    groups = lax.axis_size("dp")
    owners = lax.axis_size("expert")
    group_index = lax.axis_index("dp")
    owner_index = lax.axis_index("expert")
    local_rows = query.shape[0]
    positions_dev = kv_cache.shape[1]
    key_width = KVH * HD
    head_count = query.shape[1] // HD
    grouping = head_count // KVH
    own_heads = head_count // owners
    model_width = residual.shape[1]
    columns = model_width // owners

    outgoing = (
        lax.dynamic_slice_in_dim(fork_parent, group_index * groups, groups)
        - group_index * local_rows
    )
    out_blocks = lax.dynamic_slice_in_dim(fork_block, group_index * groups, groups)
    send_rows = jnp.where(
        (owner_index >= out_blocks)[:, None, None],
        kv_cache[outgoing],
        jnp.zeros((), kv_cache.dtype),
    )
    arrived = lax.all_to_all(send_rows, "dp", split_axis=0, concat_axis=0, tiled=True)
    incoming = jnp.arange(groups, dtype=jnp.int32) * groups + group_index
    targets = fork_child[incoming] - group_index * local_rows
    take_new = owner_index >= fork_block[incoming]
    cache = kv_cache.at[targets].set(jnp.where(take_new[:, None, None], arrived, kv_cache[targets]))

    score_scale = 1.0 / math.sqrt(HD)
    positions = owner_index * positions_dev + jnp.arange(positions_dev, dtype=jnp.int32)
    visible = positions[None, :] < lengths[:, None]
    cached_keys = cache[:, :, :key_width].reshape(local_rows, positions_dev, KVH, HD)
    cached_values = cache[:, :, key_width:].reshape(local_rows, positions_dev, KVH, HD)
    grouped = query.reshape(local_rows, KVH, grouping, HD)
    scores = (
        jnp.einsum("bkgd,bpkd->bkgp", grouped, cached_keys, preferred_element_type=jnp.float32)
        * score_scale
    )
    scores = jnp.where(visible[:, None, None, :], scores, -1e30)
    highest = jnp.max(scores, axis=3)
    weights = jnp.where(visible[:, None, None, :], jnp.exp(scores - highest[..., None]), 0.0)
    weight_sum = jnp.sum(weights, axis=3)
    partial_out = jnp.einsum(
        "bkgp,bpkd->bkgd",
        weights.astype(jnp.bfloat16),
        cached_values,
        preferred_element_type=jnp.float32,
    )

    head_block = local_rows * own_heads
    send_out = partial_out.reshape(local_rows, owners, own_heads, HD).transpose(1, 0, 2, 3)
    send_peak = highest.reshape(local_rows, owners, own_heads).transpose(1, 0, 2)
    send_sum = weight_sum.reshape(local_rows, owners, own_heads).transpose(1, 0, 2)
    stats = jnp.stack([send_peak, send_sum], axis=1).reshape(owners, 2 * head_block)
    stat_parts = split_three(stats).transpose(1, 0, 2).reshape(owners, 6 * head_block)
    stat_width = -(-6 * head_block // HD) * HD
    stat_parts = jnp.pad(stat_parts, ((0, 0), (0, stat_width - 6 * head_block)))
    packed = jnp.concatenate(
        [
            send_out.astype(jnp.bfloat16).reshape(owners, head_block, HD),
            stat_parts.reshape(owners, stat_width // HD, HD),
        ],
        axis=1,
    )
    got = spread_to_owners(packed, "expert")
    got_out = got[:, :head_block].astype(jnp.float32).reshape(owners, local_rows, own_heads, HD)
    got_stats = got[:, head_block:].reshape(owners, stat_width)[:, : 6 * head_block]
    got_stats = got_stats.reshape(owners, 3, 2 * head_block).astype(jnp.float32)
    got_stats = (got_stats[:, 0] + got_stats[:, 1]) + got_stats[:, 2]
    got_stats = got_stats.reshape(owners, 2, local_rows, own_heads)
    got_peak = got_stats[:, 0]
    got_sum = got_stats[:, 1]
    head_peak = jnp.max(got_peak, axis=0)
    factors = jnp.exp(got_peak - head_peak[None])
    head_out = jnp.sum(got_out * factors[..., None], axis=0)
    head_sum = jnp.sum(got_sum * factors, axis=0)

    own_query = lax.dynamic_slice_in_dim(query, owner_index * own_heads * HD, own_heads * HD, 1)
    own_query = own_query.reshape(local_rows, own_heads, HD).astype(jnp.float32)
    kv_index = (owner_index * own_heads + jnp.arange(own_heads, dtype=jnp.int32)) // grouping
    new_keys = jnp.take(
        new_kv[:, :key_width].reshape(local_rows, KVH, HD), kv_index, axis=1
    ).astype(jnp.float32)
    new_values = jnp.take(
        new_kv[:, key_width:].reshape(local_rows, KVH, HD), kv_index, axis=1
    ).astype(jnp.float32)
    own_score = jnp.sum(own_query * new_keys, axis=2) * score_scale
    new_peak = jnp.maximum(head_peak, own_score)
    old_factor = jnp.exp(head_peak - new_peak)
    own_weight = jnp.exp(own_score - new_peak)
    denominator = head_sum * old_factor + own_weight
    own_rounded = lax.optimization_barrier(own_weight.astype(jnp.bfloat16)).astype(jnp.float32)
    attended = (
        head_out * old_factor[..., None] + own_rounded[..., None] * new_values
    ) / denominator[..., None]
    attended = attended.astype(jnp.bfloat16).reshape(local_rows, own_heads * HD)

    proj_blocks = jnp.einsum(
        "bd,doc->obc",
        attended,
        out_weight.reshape(own_heads * HD, owners, columns),
        preferred_element_type=jnp.float32,
    )
    got_proj = spread_to_owners(proj_blocks.astype(jnp.bfloat16), "expert")
    projected_cols = jnp.sum(got_proj.astype(jnp.float32), axis=0)
    attn_cols = projected_cols.astype(jnp.bfloat16)
    residual_cols = lax.dynamic_slice_in_dim(residual, owner_index * columns, columns, 1)
    stream_cols = residual_cols.astype(jnp.float32) + projected_cols

    top_k = route_ids.shape[1]
    experts_total = w_gate.shape[0] * owners
    capacity = max(2, 2 * local_rows * top_k // experts_total)
    own_ids = lax.dynamic_slice_in_dim(route_ids, group_index * local_rows, local_rows, 0)
    own_gates = lax.dynamic_slice_in_dim(route_weights, group_index * local_rows, local_rows, 0)
    expert_ids = jnp.arange(experts_total, dtype=jnp.int32)
    matched = (own_ids[:, :, None] == expert_ids[None, None, :]).astype(jnp.int32)
    flat_matched = matched.reshape(local_rows * top_k, experts_total)
    ranking = jnp.cumsum(flat_matched, axis=0) - 1
    slot_ids = jnp.arange(capacity, dtype=jnp.int32)
    hit = (flat_matched[:, :, None] == 1) & (ranking[:, :, None] == slot_ids[None, None, :])
    hit = hit.astype(jnp.int32).reshape(local_rows, top_k, experts_total, capacity)
    slot_weight = jnp.sum(hit.astype(jnp.float32) * own_gates[:, :, None, None], axis=1)
    slot_token = jnp.sum(hit, axis=1)
    token_ids = jnp.arange(local_rows, dtype=jnp.int32)
    slot_source = jnp.sum(slot_token * token_ids[:, None, None], axis=0)
    slot_used = jnp.sum(slot_token, axis=0) > 0

    slot_cols = jnp.where(slot_used[:, :, None], stream_cols[slot_source], 0.0).astype(jnp.bfloat16)
    slot_cols = jnp.broadcast_to(slot_cols[None], (groups,) + slot_cols.shape)
    slot_cols = slot_cols.reshape(groups * experts_total, capacity, columns)
    rows_in = spread_to_owners(slot_cols, ("dp", "expert"))
    rows_in = rows_in.reshape(groups, owners, capacity, columns).transpose(0, 2, 1, 3)
    stream_rows = rows_in.reshape(groups * capacity, model_width).astype(jnp.float32)
    inverse = lax.rsqrt(
        jnp.sum(stream_rows * stream_rows, axis=1, keepdims=True) / model_width + 1e-06
    )
    piece = (stream_rows * inverse).astype(jnp.bfloat16)
    gate_proj = jnp.dot(piece, w_gate[0], preferred_element_type=jnp.float32)
    up_proj = jnp.dot(piece, w_up[0], preferred_element_type=jnp.float32)
    hidden = (jax.nn.silu(gate_proj) * up_proj).astype(jnp.bfloat16)
    outputs = jnp.dot(hidden, w_down[0], preferred_element_type=jnp.float32)

    out_blocks = outputs.astype(jnp.bfloat16).reshape(groups, capacity, owners, columns)
    out_blocks = out_blocks.transpose(0, 2, 1, 3).reshape(groups * owners, capacity, columns)
    partials = spread_to_owners(out_blocks, ("dp", "expert"))
    partials = partials.reshape(groups, experts_total, capacity, columns)
    summed = jnp.sum(partials.astype(jnp.float32), axis=0)
    mix_cols = jnp.einsum(
        "tes,esc->tc", slot_weight, summed, precision=lax.Precision.HIGHEST
    ).astype(jnp.bfloat16)
    return (attn_cols, mix_cols)


def solution(mesh):
    in_specs = (
        P("dp", None),
        P("dp", None),
        P("dp", "expert", None),
        P("dp"),
        P(),
        P(),
        P(),
        P("expert", None),
        P("dp", None),
        P(),
        P(),
        P("expert", None, "dp"),
        P("expert", None, "dp"),
        P("expert", "dp", None),
    )
    out_specs = (P("dp", "expert"), P("dp", "expert"))
    return jax.shard_map(shards, mesh=mesh, in_specs=in_specs, out_specs=out_specs, check_vma=False)
```

```python
import math

import jax
import jax.numpy as jnp
from jax import lax
from jax.sharding import PartitionSpec as P

HD = 128
KVH = 4


def spread_to_owners(blocks, axis):
    return lax.all_to_all(blocks, axis, 0, 0, tiled=True)


def split_three(values):
    high = lax.reduce_precision(values, exponent_bits=8, mantissa_bits=7)
    rest = values - high
    middle = lax.reduce_precision(rest, exponent_bits=8, mantissa_bits=7)
    low = rest - middle
    return jnp.stack([high, middle, low]).astype(jnp.bfloat16)


def shards(
    query,
    new_kv,
    kv_cache,
    lengths,
    fork_parent,
    fork_child,
    fork_block,
    out_weight,
    residual,
    route_ids,
    route_weights,
    w_gate,
    w_up,
    w_down,
):
    groups = lax.axis_size("dp")
    owners = lax.axis_size("expert")
    group_index = lax.axis_index("dp")
    owner_index = lax.axis_index("expert")
    local_rows = query.shape[0]
    positions_dev = kv_cache.shape[1]
    key_width = KVH * HD
    head_count = query.shape[1] // HD
    grouping = head_count // KVH
    own_heads = head_count // owners
    model_width = residual.shape[1]
    columns = model_width // owners

    outgoing = (
        lax.dynamic_slice_in_dim(fork_parent, group_index * groups, groups)
        - group_index * local_rows
    )
    out_blocks = lax.dynamic_slice_in_dim(fork_block, group_index * groups, groups)
    send_rows = jnp.where(
        (owner_index >= out_blocks)[:, None, None],
        kv_cache[outgoing],
        jnp.zeros((), kv_cache.dtype),
    )
    fork_shape = send_rows.shape
    send_rows = send_rows.reshape(fork_shape[0], fork_shape[1] // 2, 2 * fork_shape[2])
    arrived = spread_to_owners(send_rows, "dp").reshape(fork_shape)
    incoming = jnp.arange(groups, dtype=jnp.int32) * groups + group_index
    targets = fork_child[incoming] - group_index * local_rows
    take_new = owner_index >= fork_block[incoming]
    cache = kv_cache.at[targets].set(jnp.where(take_new[:, None, None], arrived, kv_cache[targets]))

    score_scale = 1.0 / math.sqrt(HD)
    positions = owner_index * positions_dev + jnp.arange(positions_dev, dtype=jnp.int32)
    visible = positions[None, :] < lengths[:, None]
    cached_keys = cache[:, :, :key_width].reshape(local_rows, positions_dev, KVH, HD)
    cached_values = cache[:, :, key_width:].reshape(local_rows, positions_dev, KVH, HD)
    grouped = query.reshape(local_rows, KVH, grouping, HD)
    scores = (
        jnp.einsum("bkgd,bpkd->bkgp", grouped, cached_keys, preferred_element_type=jnp.float32)
        * score_scale
    )
    scores = jnp.where(visible[:, None, None, :], scores, -1e30)
    highest = jnp.max(scores, axis=3)
    weights = jnp.where(visible[:, None, None, :], jnp.exp(scores - highest[..., None]), 0.0)
    weight_sum = jnp.sum(weights, axis=3)
    partial_out = jnp.einsum(
        "bkgp,bpkd->bkgd",
        weights.astype(jnp.bfloat16),
        cached_values,
        preferred_element_type=jnp.float32,
    )

    head_block = local_rows * own_heads
    send_out = partial_out.reshape(local_rows, owners, own_heads, HD).transpose(1, 0, 2, 3)
    send_peak = highest.reshape(local_rows, owners, own_heads).transpose(1, 0, 2)
    send_sum = weight_sum.reshape(local_rows, owners, own_heads).transpose(1, 0, 2)
    stats = jnp.stack([send_peak, send_sum], axis=1).reshape(owners, 2 * head_block)
    stat_parts = split_three(stats).transpose(1, 0, 2).reshape(owners, 6 * head_block)
    stat_width = -(-6 * head_block // HD) * HD
    stat_parts = jnp.pad(stat_parts, ((0, 0), (0, stat_width - 6 * head_block)))
    packed = jnp.concatenate(
        [
            send_out.astype(jnp.bfloat16).reshape(owners, head_block, HD),
            stat_parts.reshape(owners, stat_width // HD, HD),
        ],
        axis=1,
    )
    got = spread_to_owners(packed, "expert")
    got_out = got[:, :head_block].astype(jnp.float32).reshape(owners, local_rows, own_heads, HD)
    got_stats = got[:, head_block:].reshape(owners, stat_width)[:, : 6 * head_block]
    got_stats = got_stats.reshape(owners, 3, 2 * head_block).astype(jnp.float32)
    got_stats = (got_stats[:, 0] + got_stats[:, 1]) + got_stats[:, 2]
    got_stats = got_stats.reshape(owners, 2, local_rows, own_heads)
    got_peak = got_stats[:, 0]
    got_sum = got_stats[:, 1]
    head_peak = jnp.max(got_peak, axis=0)
    factors = jnp.exp(got_peak - head_peak[None])
    head_out = jnp.sum(got_out * factors[..., None], axis=0)
    head_sum = jnp.sum(got_sum * factors, axis=0)

    own_query = lax.dynamic_slice_in_dim(query, owner_index * own_heads * HD, own_heads * HD, 1)
    own_query = own_query.reshape(local_rows, own_heads, HD).astype(jnp.float32)
    kv_index = (owner_index * own_heads + jnp.arange(own_heads, dtype=jnp.int32)) // grouping
    new_keys = jnp.take(
        new_kv[:, :key_width].reshape(local_rows, KVH, HD), kv_index, axis=1
    ).astype(jnp.float32)
    new_values = jnp.take(
        new_kv[:, key_width:].reshape(local_rows, KVH, HD), kv_index, axis=1
    ).astype(jnp.float32)
    own_score = jnp.sum(own_query * new_keys, axis=2) * score_scale
    new_peak = jnp.maximum(head_peak, own_score)
    old_factor = jnp.exp(head_peak - new_peak)
    own_weight = jnp.exp(own_score - new_peak)
    denominator = head_sum * old_factor + own_weight
    own_rounded = lax.optimization_barrier(own_weight.astype(jnp.bfloat16)).astype(jnp.float32)
    attended = (
        head_out * old_factor[..., None] + own_rounded[..., None] * new_values
    ) / denominator[..., None]
    attended = attended.astype(jnp.bfloat16).reshape(local_rows, own_heads * HD)

    proj_blocks = jnp.einsum(
        "bd,doc->obc",
        attended,
        out_weight.reshape(own_heads * HD, owners, columns),
        preferred_element_type=jnp.float32,
    )
    got_proj = spread_to_owners(proj_blocks.astype(jnp.bfloat16), "expert")
    projected_cols = jnp.sum(got_proj.astype(jnp.float32), axis=0)
    attn_cols = projected_cols.astype(jnp.bfloat16)
    residual_cols = lax.dynamic_slice_in_dim(residual, owner_index * columns, columns, 1)
    stream_cols = residual_cols.astype(jnp.float32) + projected_cols

    top_k = route_ids.shape[1]
    experts_total = w_gate.shape[0] * owners
    capacity = max(2, 2 * local_rows * top_k // experts_total)
    own_ids = lax.dynamic_slice_in_dim(route_ids, group_index * local_rows, local_rows, 0)
    own_gates = lax.dynamic_slice_in_dim(route_weights, group_index * local_rows, local_rows, 0)
    expert_ids = jnp.arange(experts_total, dtype=jnp.int32)
    matched = (own_ids[:, :, None] == expert_ids[None, None, :]).astype(jnp.int32)
    flat_matched = matched.reshape(local_rows * top_k, experts_total)
    ranking = jnp.cumsum(flat_matched, axis=0) - 1
    slot_ids = jnp.arange(capacity, dtype=jnp.int32)
    hit = (flat_matched[:, :, None] == 1) & (ranking[:, :, None] == slot_ids[None, None, :])
    hit = hit.astype(jnp.int32).reshape(local_rows, top_k, experts_total, capacity)
    slot_weight = jnp.sum(hit.astype(jnp.float32) * own_gates[:, :, None, None], axis=1)
    slot_token = jnp.sum(hit, axis=1)
    token_ids = jnp.arange(local_rows, dtype=jnp.int32)
    slot_source = jnp.sum(slot_token * token_ids[:, None, None], axis=0)
    slot_used = jnp.sum(slot_token, axis=0) > 0

    slot_cols = jnp.where(slot_used[:, :, None], stream_cols[slot_source], 0.0).astype(jnp.bfloat16)
    slot_cols = jnp.broadcast_to(slot_cols[None], (groups,) + slot_cols.shape)
    slot_cols = slot_cols.reshape(groups * experts_total, capacity, columns)
    rows_in = spread_to_owners(slot_cols, ("dp", "expert"))
    rows_in = rows_in.reshape(groups, owners, capacity, columns).transpose(0, 2, 1, 3)
    stream_rows = rows_in.reshape(groups * capacity, model_width).astype(jnp.float32)
    inverse = lax.rsqrt(
        jnp.sum(stream_rows * stream_rows, axis=1, keepdims=True) / model_width + 1e-06
    )
    piece = (stream_rows * inverse).astype(jnp.bfloat16)
    gate_proj = jnp.dot(piece, w_gate[0], preferred_element_type=jnp.float32)
    up_proj = jnp.dot(piece, w_up[0], preferred_element_type=jnp.float32)
    hidden = (jax.nn.silu(gate_proj) * up_proj).astype(jnp.bfloat16)
    outputs = jnp.dot(hidden, w_down[0], preferred_element_type=jnp.float32)

    out_blocks = outputs.astype(jnp.bfloat16).reshape(groups, capacity, owners, columns)
    out_blocks = out_blocks.transpose(0, 2, 1, 3).reshape(groups * owners, capacity, columns)
    partials = spread_to_owners(out_blocks, ("dp", "expert"))
    partials = partials.reshape(groups, experts_total, capacity, columns)
    summed = jnp.sum(partials.astype(jnp.float32), axis=0)
    mix_cols = jnp.einsum(
        "tes,esc->tc", slot_weight, summed, precision=lax.Precision.HIGHEST
    ).astype(jnp.bfloat16)
    return (attn_cols, mix_cols)


def solution(mesh):
    in_specs = (
        P("dp", None),
        P("dp", None),
        P("dp", "expert", None),
        P("dp"),
        P(),
        P(),
        P(),
        P("expert", None),
        P("dp", None),
        P(),
        P(),
        P("expert", None, "dp"),
        P("expert", None, "dp"),
        P("expert", "dp", None),
    )
    out_specs = (P("dp", "expert"), P("dp", "expert"))
    return jax.shard_map(shards, mesh=mesh, in_specs=in_specs, out_specs=out_specs, check_vma=False)
```

```python
import math

import jax
import jax.numpy as jnp
from jax import lax
from jax.sharding import PartitionSpec as P

HD = 128
KVH = 4


def spread_to_owners(blocks, axis):
    return lax.all_to_all(blocks, axis, 0, 0, tiled=True)


def split_three(values):
    high = lax.reduce_precision(values, exponent_bits=8, mantissa_bits=7)
    rest = values - high
    middle = lax.reduce_precision(rest, exponent_bits=8, mantissa_bits=7)
    low = rest - middle
    return jnp.stack([high, middle, low]).astype(jnp.bfloat16)


def shards(
    query,
    new_kv,
    kv_cache,
    lengths,
    fork_parent,
    fork_child,
    fork_block,
    out_weight,
    residual,
    route_ids,
    route_weights,
    w_gate,
    w_up,
    w_down,
):
    groups = lax.axis_size("dp")
    owners = lax.axis_size("expert")
    group_index = lax.axis_index("dp")
    owner_index = lax.axis_index("expert")
    local_rows = query.shape[0]
    positions_dev = kv_cache.shape[1]
    key_width = KVH * HD
    head_count = query.shape[1] // HD
    grouping = head_count // KVH
    own_heads = head_count // owners
    model_width = residual.shape[1]
    columns = model_width // owners

    outgoing = (
        lax.dynamic_slice_in_dim(fork_parent, group_index * groups, groups)
        - group_index * local_rows
    )
    send_rows = kv_cache[outgoing]
    fork_shape = send_rows.shape
    send_rows = send_rows.reshape(fork_shape[0], fork_shape[1] // 2, 2 * fork_shape[2])
    arrived = spread_to_owners(send_rows, "dp").reshape(fork_shape)
    incoming = jnp.arange(groups, dtype=jnp.int32) * groups + group_index
    targets = fork_child[incoming] - group_index * local_rows
    take_new = owner_index >= fork_block[incoming]
    cache = kv_cache.at[targets].set(jnp.where(take_new[:, None, None], arrived, kv_cache[targets]))

    score_scale = 1.0 / math.sqrt(HD)
    positions = owner_index * positions_dev + jnp.arange(positions_dev, dtype=jnp.int32)
    visible = positions[None, :] < lengths[:, None]
    cached_keys = cache[:, :, :key_width].reshape(local_rows, positions_dev, KVH, HD)
    cached_values = cache[:, :, key_width:].reshape(local_rows, positions_dev, KVH, HD)
    grouped = query.reshape(local_rows, KVH, grouping, HD)
    scores = (
        jnp.einsum("bkgd,bpkd->bkgp", grouped, cached_keys, preferred_element_type=jnp.float32)
        * score_scale
    )
    scores = jnp.where(visible[:, None, None, :], scores, -1e30)
    highest = jnp.max(scores, axis=3)
    weights = jnp.where(visible[:, None, None, :], jnp.exp(scores - highest[..., None]), 0.0)
    weight_sum = jnp.sum(weights, axis=3)
    partial_out = jnp.einsum(
        "bkgp,bpkd->bkgd",
        weights.astype(jnp.bfloat16),
        cached_values,
        preferred_element_type=jnp.float32,
    )

    head_block = local_rows * own_heads
    send_out = partial_out.reshape(local_rows, owners, own_heads, HD).transpose(1, 0, 2, 3)
    send_peak = highest.reshape(local_rows, owners, own_heads).transpose(1, 0, 2)
    send_sum = weight_sum.reshape(local_rows, owners, own_heads).transpose(1, 0, 2)
    stats = jnp.stack([send_peak, send_sum], axis=1).reshape(owners, 2 * head_block)
    stat_parts = split_three(stats).transpose(1, 0, 2).reshape(owners, 6 * head_block)
    stat_width = -(-6 * head_block // HD) * HD
    stat_parts = jnp.pad(stat_parts, ((0, 0), (0, stat_width - 6 * head_block)))
    packed = jnp.concatenate(
        [
            send_out.astype(jnp.bfloat16).reshape(owners, head_block, HD),
            stat_parts.reshape(owners, stat_width // HD, HD),
        ],
        axis=1,
    )
    got = spread_to_owners(packed, "expert")
    got_out = got[:, :head_block].astype(jnp.float32).reshape(owners, local_rows, own_heads, HD)
    got_stats = got[:, head_block:].reshape(owners, stat_width)[:, : 6 * head_block]
    got_stats = got_stats.reshape(owners, 3, 2 * head_block).astype(jnp.float32)
    got_stats = (got_stats[:, 0] + got_stats[:, 1]) + got_stats[:, 2]
    got_stats = got_stats.reshape(owners, 2, local_rows, own_heads)
    got_peak = got_stats[:, 0]
    got_sum = got_stats[:, 1]
    head_peak = jnp.max(got_peak, axis=0)
    factors = jnp.exp(got_peak - head_peak[None])
    head_out = jnp.sum(got_out * factors[..., None], axis=0)
    head_sum = jnp.sum(got_sum * factors, axis=0)

    own_query = lax.dynamic_slice_in_dim(query, owner_index * own_heads * HD, own_heads * HD, 1)
    own_query = own_query.reshape(local_rows, own_heads, HD).astype(jnp.float32)
    kv_index = (owner_index * own_heads + jnp.arange(own_heads, dtype=jnp.int32)) // grouping
    new_keys = jnp.take(
        new_kv[:, :key_width].reshape(local_rows, KVH, HD), kv_index, axis=1
    ).astype(jnp.float32)
    new_values = jnp.take(
        new_kv[:, key_width:].reshape(local_rows, KVH, HD), kv_index, axis=1
    ).astype(jnp.float32)
    own_score = jnp.sum(own_query * new_keys, axis=2) * score_scale
    new_peak = jnp.maximum(head_peak, own_score)
    old_factor = jnp.exp(head_peak - new_peak)
    own_weight = jnp.exp(own_score - new_peak)
    denominator = head_sum * old_factor + own_weight
    own_rounded = lax.optimization_barrier(own_weight.astype(jnp.bfloat16)).astype(jnp.float32)
    attended = (
        head_out * old_factor[..., None] + own_rounded[..., None] * new_values
    ) / denominator[..., None]
    attended = attended.astype(jnp.bfloat16).reshape(local_rows, own_heads * HD)

    proj_blocks = jnp.einsum(
        "bd,doc->obc",
        attended,
        out_weight.reshape(own_heads * HD, owners, columns),
        preferred_element_type=jnp.float32,
    )
    got_proj = spread_to_owners(proj_blocks.astype(jnp.bfloat16), "expert")
    projected_cols = jnp.sum(got_proj.astype(jnp.float32), axis=0)
    attn_cols = projected_cols.astype(jnp.bfloat16)
    residual_cols = lax.dynamic_slice_in_dim(residual, owner_index * columns, columns, 1)
    stream_cols = residual_cols.astype(jnp.float32) + projected_cols

    top_k = route_ids.shape[1]
    experts_total = w_gate.shape[0] * owners
    capacity = max(2, 2 * local_rows * top_k // experts_total)
    own_ids = lax.dynamic_slice_in_dim(route_ids, group_index * local_rows, local_rows, 0)
    own_gates = lax.dynamic_slice_in_dim(route_weights, group_index * local_rows, local_rows, 0)
    expert_ids = jnp.arange(experts_total, dtype=jnp.int32)
    matched = (own_ids[:, :, None] == expert_ids[None, None, :]).astype(jnp.int32)
    flat_matched = matched.reshape(local_rows * top_k, experts_total)
    ranking = jnp.cumsum(flat_matched, axis=0) - 1
    slot_ids = jnp.arange(capacity, dtype=jnp.int32)
    hit = (flat_matched[:, :, None] == 1) & (ranking[:, :, None] == slot_ids[None, None, :])
    hit = hit.astype(jnp.int32).reshape(local_rows, top_k, experts_total, capacity)
    slot_weight = jnp.sum(hit.astype(jnp.float32) * own_gates[:, :, None, None], axis=1)
    slot_token = jnp.sum(hit, axis=1)
    token_ids = jnp.arange(local_rows, dtype=jnp.int32)
    slot_source = jnp.sum(slot_token * token_ids[:, None, None], axis=0)
    slot_used = jnp.sum(slot_token, axis=0) > 0

    slot_cols = jnp.where(slot_used[:, :, None], stream_cols[slot_source], 0.0).astype(jnp.bfloat16)
    slot_cols = jnp.broadcast_to(slot_cols[None], (groups,) + slot_cols.shape)
    slot_cols = slot_cols.reshape(groups * experts_total, capacity, columns)
    rows_in = spread_to_owners(slot_cols, ("dp", "expert"))
    rows_in = rows_in.reshape(groups, owners, capacity, columns).astype(jnp.float32)
    inverse = lax.rsqrt(
        jnp.sum(rows_in * rows_in, axis=(1, 3), keepdims=True) / model_width + 1e-06
    )
    piece = (rows_in * inverse).astype(jnp.bfloat16)
    hidden_width = w_gate.shape[2]
    gate_proj = jnp.einsum(
        "gosc,ocf->gsf",
        piece,
        w_gate[0].reshape(owners, columns, hidden_width),
        preferred_element_type=jnp.float32,
    )
    up_proj = jnp.einsum(
        "gosc,ocf->gsf",
        piece,
        w_up[0].reshape(owners, columns, hidden_width),
        preferred_element_type=jnp.float32,
    )
    hidden = (jax.nn.silu(gate_proj) * up_proj).astype(jnp.bfloat16)
    outputs = jnp.einsum(
        "gsf,foc->gosc",
        hidden,
        w_down[0].reshape(hidden_width, owners, columns),
        preferred_element_type=jnp.float32,
    )

    out_blocks = outputs.astype(jnp.bfloat16).reshape(groups * owners, capacity, columns)
    partials = spread_to_owners(out_blocks, ("dp", "expert"))
    partials = partials.reshape(groups, experts_total, capacity, columns)
    summed = jnp.sum(partials.astype(jnp.float32), axis=0)
    mix_cols = jnp.einsum(
        "tes,esc->tc", slot_weight, summed, precision=lax.Precision.HIGHEST
    ).astype(jnp.bfloat16)
    return (attn_cols, mix_cols)


def solution(mesh):
    in_specs = (
        P("dp", None),
        P("dp", None),
        P("dp", "expert", None),
        P("dp"),
        P(),
        P(),
        P(),
        P("expert", None),
        P("dp", None),
        P(),
        P(),
        P("expert", None, "dp"),
        P("expert", None, "dp"),
        P("expert", "dp", None),
    )
    out_specs = (P("dp", "expert"), P("dp", "expert"))
    return jax.shard_map(shards, mesh=mesh, in_specs=in_specs, out_specs=out_specs, check_vma=False)
```

```python
import math

import jax
import jax.numpy as jnp
from jax import lax
from jax.sharding import PartitionSpec as P

HD = 128
KVH = 4


def spread_to_owners(blocks, axis):
    return lax.all_to_all(blocks, axis, 0, 0, tiled=True)


def split_three(values):
    high = lax.reduce_precision(values, exponent_bits=8, mantissa_bits=7)
    rest = values - high
    middle = lax.reduce_precision(rest, exponent_bits=8, mantissa_bits=7)
    low = rest - middle
    return jnp.stack([high, middle, low]).astype(jnp.bfloat16)


def shards(
    query,
    new_kv,
    kv_cache,
    lengths,
    fork_parent,
    fork_child,
    fork_block,
    out_weight,
    residual,
    route_ids,
    route_weights,
    w_gate,
    w_up,
    w_down,
):
    groups = lax.axis_size("dp")
    owners = lax.axis_size("expert")
    group_index = lax.axis_index("dp")
    owner_index = lax.axis_index("expert")
    local_rows = query.shape[0]
    positions_dev = kv_cache.shape[1]
    key_width = KVH * HD
    head_count = query.shape[1] // HD
    grouping = head_count // KVH
    own_heads = head_count // owners
    model_width = residual.shape[1]
    columns = model_width // owners

    outgoing = (
        lax.dynamic_slice_in_dim(fork_parent, group_index * groups, groups)
        - group_index * local_rows
    )
    send_rows = kv_cache[outgoing]
    fork_shape = send_rows.shape
    send_rows = send_rows.reshape(fork_shape[0], fork_shape[1] // 2, 2 * fork_shape[2])
    arrived = spread_to_owners(send_rows, "dp").reshape(fork_shape)
    incoming = jnp.arange(groups, dtype=jnp.int32) * groups + group_index
    targets = fork_child[incoming] - group_index * local_rows
    take_new = owner_index >= fork_block[incoming]
    cache = kv_cache.at[targets].set(jnp.where(take_new[:, None, None], arrived, kv_cache[targets]))

    score_scale = 1.0 / math.sqrt(HD)
    positions = owner_index * positions_dev + jnp.arange(positions_dev, dtype=jnp.int32)
    visible = positions[None, :] < lengths[:, None]
    cached_keys = cache[:, :, :key_width].reshape(local_rows, positions_dev, KVH, HD)
    cached_values = cache[:, :, key_width:].reshape(local_rows, positions_dev, KVH, HD)
    grouped = query.reshape(local_rows, KVH, grouping, HD)
    scores = (
        jnp.einsum("bkgd,bpkd->bkgp", grouped, cached_keys, preferred_element_type=jnp.float32)
        * score_scale
    )
    scores = jnp.where(visible[:, None, None, :], scores, -1e30)
    highest = jnp.max(scores, axis=3)
    weights = jnp.where(visible[:, None, None, :], jnp.exp(scores - highest[..., None]), 0.0)
    weight_sum = jnp.sum(weights, axis=3)
    partial_out = jnp.einsum(
        "bkgp,bpkd->bkgd",
        weights.astype(jnp.bfloat16),
        cached_values,
        preferred_element_type=jnp.float32,
    )

    head_block = local_rows * own_heads
    send_out = partial_out.reshape(local_rows, owners, own_heads, HD).transpose(1, 0, 2, 3)
    send_peak = highest.reshape(local_rows, owners, own_heads).transpose(1, 0, 2)
    send_sum = weight_sum.reshape(local_rows, owners, own_heads).transpose(1, 0, 2)
    stats = jnp.stack([send_peak, send_sum], axis=1).reshape(owners, 2 * head_block)
    stat_parts = split_three(stats).transpose(1, 0, 2).reshape(owners, 6 * head_block)
    stat_width = -(-6 * head_block // HD) * HD
    stat_parts = jnp.pad(stat_parts, ((0, 0), (0, stat_width - 6 * head_block)))
    packed = jnp.concatenate(
        [send_out.astype(jnp.bfloat16).reshape(owners, head_block * HD), stat_parts], axis=1
    )
    got = spread_to_owners(packed[:, None], "expert")[:, 0]
    got_out = got[:, : head_block * HD].astype(jnp.float32)
    got_out = got_out.reshape(owners, local_rows, own_heads, HD)
    got_stats = got[:, head_block * HD : head_block * HD + 6 * head_block]
    got_stats = got_stats.reshape(owners, 3, 2 * head_block).astype(jnp.float32)
    got_stats = (got_stats[:, 0] + got_stats[:, 1]) + got_stats[:, 2]
    got_stats = got_stats.reshape(owners, 2, local_rows, own_heads)
    got_peak = got_stats[:, 0]
    got_sum = got_stats[:, 1]
    head_peak = jnp.max(got_peak, axis=0)
    factors = jnp.exp(got_peak - head_peak[None])
    head_out = jnp.sum(got_out * factors[..., None], axis=0)
    head_sum = jnp.sum(got_sum * factors, axis=0)

    own_query = lax.dynamic_slice_in_dim(query, owner_index * own_heads * HD, own_heads * HD, 1)
    own_query = own_query.reshape(local_rows, own_heads, HD).astype(jnp.float32)
    kv_index = (owner_index * own_heads + jnp.arange(own_heads, dtype=jnp.int32)) // grouping
    new_keys = jnp.take(
        new_kv[:, :key_width].reshape(local_rows, KVH, HD), kv_index, axis=1
    ).astype(jnp.float32)
    new_values = jnp.take(
        new_kv[:, key_width:].reshape(local_rows, KVH, HD), kv_index, axis=1
    ).astype(jnp.float32)
    own_score = jnp.sum(own_query * new_keys, axis=2) * score_scale
    new_peak = jnp.maximum(head_peak, own_score)
    old_factor = jnp.exp(head_peak - new_peak)
    own_weight = jnp.exp(own_score - new_peak)
    denominator = head_sum * old_factor + own_weight
    own_rounded = lax.optimization_barrier(own_weight.astype(jnp.bfloat16)).astype(jnp.float32)
    attended = (
        head_out * old_factor[..., None] + own_rounded[..., None] * new_values
    ) / denominator[..., None]
    attended = attended.astype(jnp.bfloat16).reshape(local_rows, own_heads * HD)

    proj_blocks = jnp.einsum(
        "bd,doc->obc",
        attended,
        out_weight.reshape(own_heads * HD, owners, columns),
        preferred_element_type=jnp.float32,
    )
    got_proj = spread_to_owners(proj_blocks.astype(jnp.bfloat16), "expert")
    projected_cols = jnp.sum(got_proj.astype(jnp.float32), axis=0)
    attn_cols = projected_cols.astype(jnp.bfloat16)
    residual_cols = lax.dynamic_slice_in_dim(residual, owner_index * columns, columns, 1)
    stream_cols = residual_cols.astype(jnp.float32) + projected_cols

    top_k = route_ids.shape[1]
    experts_total = w_gate.shape[0] * owners
    capacity = max(2, 2 * local_rows * top_k // experts_total)
    own_ids = lax.dynamic_slice_in_dim(route_ids, group_index * local_rows, local_rows, 0)
    own_gates = lax.dynamic_slice_in_dim(route_weights, group_index * local_rows, local_rows, 0)
    expert_ids = jnp.arange(experts_total, dtype=jnp.int32)
    matched = (own_ids[:, :, None] == expert_ids[None, None, :]).astype(jnp.int32)
    flat_matched = matched.reshape(local_rows * top_k, experts_total)
    ranking = jnp.cumsum(flat_matched, axis=0) - 1
    slot_ids = jnp.arange(capacity, dtype=jnp.int32)
    hit = (flat_matched[:, :, None] == 1) & (ranking[:, :, None] == slot_ids[None, None, :])
    hit = hit.astype(jnp.int32).reshape(local_rows, top_k, experts_total, capacity)
    slot_weight = jnp.sum(hit.astype(jnp.float32) * own_gates[:, :, None, None], axis=1)
    slot_token = jnp.sum(hit, axis=1)
    token_ids = jnp.arange(local_rows, dtype=jnp.int32)
    slot_source = jnp.sum(slot_token * token_ids[:, None, None], axis=0)
    slot_used = jnp.sum(slot_token, axis=0) > 0

    slot_cols = jnp.where(slot_used[:, :, None], stream_cols[slot_source], 0.0).astype(jnp.bfloat16)
    slot_cols = jnp.broadcast_to(slot_cols[None], (groups,) + slot_cols.shape)
    slot_cols = slot_cols.reshape(groups * experts_total, capacity, columns)
    rows_in = spread_to_owners(slot_cols, ("dp", "expert"))
    rows_in = rows_in.reshape(groups, owners, capacity, columns).transpose(0, 2, 1, 3)
    stream_rows = rows_in.reshape(groups * capacity, model_width).astype(jnp.float32)
    inverse = lax.rsqrt(
        jnp.sum(stream_rows * stream_rows, axis=1, keepdims=True) / model_width + 1e-06
    )
    piece = (stream_rows * inverse).astype(jnp.bfloat16)
    gate_proj = jnp.dot(piece, w_gate[0], preferred_element_type=jnp.float32)
    up_proj = jnp.dot(piece, w_up[0], preferred_element_type=jnp.float32)
    hidden = (jax.nn.silu(gate_proj) * up_proj).astype(jnp.bfloat16)
    outputs = jnp.dot(hidden, w_down[0], preferred_element_type=jnp.float32)

    out_blocks = outputs.astype(jnp.bfloat16).reshape(groups, capacity, owners, columns)
    out_blocks = out_blocks.transpose(0, 2, 1, 3).reshape(groups * owners, capacity, columns)
    partials = spread_to_owners(out_blocks, ("dp", "expert"))
    partials = partials.reshape(groups, experts_total, capacity, columns)
    summed = jnp.sum(partials.astype(jnp.float32), axis=0)
    mix_cols = jnp.einsum(
        "tes,esc->tc", slot_weight, summed, precision=lax.Precision.HIGHEST
    ).astype(jnp.bfloat16)
    return (attn_cols, mix_cols)


def solution(mesh):
    in_specs = (
        P("dp", None),
        P("dp", None),
        P("dp", "expert", None),
        P("dp"),
        P(),
        P(),
        P(),
        P("expert", None),
        P("dp", None),
        P(),
        P(),
        P("expert", None, "dp"),
        P("expert", None, "dp"),
        P("expert", "dp", None),
    )
    out_specs = (P("dp", "expert"), P("dp", "expert"))
    return jax.shard_map(shards, mesh=mesh, in_specs=in_specs, out_specs=out_specs, check_vma=False)
```

```python
import math

import jax
import jax.numpy as jnp
from jax import lax
from jax.sharding import PartitionSpec as P

HD = 128
KVH = 4


def spread_to_owners(blocks, axis):
    return lax.all_to_all(blocks, axis, 0, 0, tiled=True)


def split_three(values):
    high = lax.reduce_precision(values, exponent_bits=8, mantissa_bits=7)
    rest = values - high
    middle = lax.reduce_precision(rest, exponent_bits=8, mantissa_bits=7)
    low = rest - middle
    return jnp.stack([high, middle, low]).astype(jnp.bfloat16)


def shards(
    query,
    new_kv,
    kv_cache,
    lengths,
    fork_parent,
    fork_child,
    fork_block,
    out_weight,
    residual,
    route_ids,
    route_weights,
    w_gate,
    w_up,
    w_down,
):
    groups = lax.axis_size("dp")
    owners = lax.axis_size("expert")
    group_index = lax.axis_index("dp")
    owner_index = lax.axis_index("expert")
    local_rows = query.shape[0]
    positions_dev = kv_cache.shape[1]
    key_width = KVH * HD
    head_count = query.shape[1] // HD
    grouping = head_count // KVH
    own_heads = head_count // owners
    model_width = residual.shape[1]
    columns = model_width // owners

    outgoing = (
        lax.dynamic_slice_in_dim(fork_parent, group_index * groups, groups)
        - group_index * local_rows
    )
    send_rows = kv_cache[outgoing]
    fork_shape = send_rows.shape
    send_rows = send_rows.reshape(fork_shape[0], fork_shape[1] // 2, 2 * fork_shape[2])
    arrived = spread_to_owners(send_rows, "dp").reshape(fork_shape)
    incoming = jnp.arange(groups, dtype=jnp.int32) * groups + group_index
    targets = fork_child[incoming] - group_index * local_rows
    take_new = owner_index >= fork_block[incoming]
    cache = kv_cache.at[targets].set(jnp.where(take_new[:, None, None], arrived, kv_cache[targets]))

    score_scale = 1.0 / math.sqrt(HD)
    positions = owner_index * positions_dev + jnp.arange(positions_dev, dtype=jnp.int32)
    visible = positions[None, :] < lengths[:, None]
    cached_keys = cache[:, :, :key_width].reshape(local_rows, positions_dev, KVH, HD)
    cached_values = cache[:, :, key_width:].reshape(local_rows, positions_dev, KVH, HD)
    grouped = query.reshape(local_rows, KVH, grouping, HD)
    scores = (
        jnp.einsum("bkgd,bpkd->bkgp", grouped, cached_keys, preferred_element_type=jnp.float32)
        * score_scale
    )
    scores = jnp.where(visible[:, None, None, :], scores, -1e30)
    highest = jnp.max(scores, axis=3)
    weights = jnp.where(visible[:, None, None, :], jnp.exp(scores - highest[..., None]), 0.0)
    weight_sum = jnp.sum(weights, axis=3)
    partial_out = jnp.einsum(
        "bkgp,bpkd->bkgd",
        weights.astype(jnp.bfloat16),
        cached_values,
        preferred_element_type=jnp.float32,
    )

    head_block = local_rows * own_heads
    send_out = partial_out.reshape(local_rows, owners, own_heads, HD).transpose(1, 0, 2, 3)
    send_peak = highest.reshape(local_rows, owners, own_heads).transpose(1, 0, 2)
    send_sum = weight_sum.reshape(local_rows, owners, own_heads).transpose(1, 0, 2)
    stats = jnp.stack([send_peak, send_sum], axis=1).reshape(owners, 2 * head_block)
    stat_parts = split_three(stats).transpose(1, 0, 2).reshape(owners, 6 * head_block)
    stat_width = -(-6 * head_block // HD) * HD
    stat_parts = jnp.pad(stat_parts, ((0, 0), (0, stat_width - 6 * head_block)))
    packed = jnp.concatenate(
        [send_out.astype(jnp.bfloat16).reshape(owners, head_block * HD), stat_parts], axis=1
    )
    got = spread_to_owners(packed[:, None], "expert")[:, 0]
    got_out = got[:, : head_block * HD].astype(jnp.float32)
    got_out = got_out.reshape(owners, local_rows, own_heads, HD)
    got_stats = got[:, head_block * HD : head_block * HD + 6 * head_block]
    got_stats = got_stats.reshape(owners, 3, 2 * head_block).astype(jnp.float32)
    got_stats = (got_stats[:, 0] + got_stats[:, 1]) + got_stats[:, 2]
    got_stats = got_stats.reshape(owners, 2, local_rows, own_heads)
    got_peak = got_stats[:, 0]
    got_sum = got_stats[:, 1]
    head_peak = jnp.max(got_peak, axis=0)
    factors = jnp.exp(got_peak - head_peak[None])
    head_out = jnp.sum(got_out * factors[..., None], axis=0)
    head_sum = jnp.sum(got_sum * factors, axis=0)

    own_query = lax.dynamic_slice_in_dim(query, owner_index * own_heads * HD, own_heads * HD, 1)
    own_query = own_query.reshape(local_rows, own_heads, HD).astype(jnp.float32)
    kv_index = (owner_index * own_heads + jnp.arange(own_heads, dtype=jnp.int32)) // grouping
    new_keys = jnp.take(
        new_kv[:, :key_width].reshape(local_rows, KVH, HD), kv_index, axis=1
    ).astype(jnp.float32)
    new_values = jnp.take(
        new_kv[:, key_width:].reshape(local_rows, KVH, HD), kv_index, axis=1
    ).astype(jnp.float32)
    own_score = jnp.sum(own_query * new_keys, axis=2) * score_scale
    new_peak = jnp.maximum(head_peak, own_score)
    old_factor = jnp.exp(head_peak - new_peak)
    own_weight = jnp.exp(own_score - new_peak)
    denominator = head_sum * old_factor + own_weight
    own_rounded = lax.optimization_barrier(own_weight.astype(jnp.bfloat16)).astype(jnp.float32)
    attended = (
        head_out * old_factor[..., None] + own_rounded[..., None] * new_values
    ) / denominator[..., None]
    attended = attended.astype(jnp.bfloat16).reshape(local_rows, own_heads * HD)

    proj_blocks = jnp.einsum(
        "bd,doc->obc",
        attended,
        out_weight.reshape(own_heads * HD, owners, columns),
        preferred_element_type=jnp.float32,
    )
    got_proj = spread_to_owners(proj_blocks, "expert")
    projected_cols = jnp.sum(got_proj, axis=0)
    attn_cols = projected_cols.astype(jnp.bfloat16)
    residual_cols = lax.dynamic_slice_in_dim(residual, owner_index * columns, columns, 1)
    stream_cols = residual_cols.astype(jnp.float32) + projected_cols

    top_k = route_ids.shape[1]
    experts_total = w_gate.shape[0] * owners
    capacity = max(2, 2 * local_rows * top_k // experts_total)
    own_ids = lax.dynamic_slice_in_dim(route_ids, group_index * local_rows, local_rows, 0)
    own_gates = lax.dynamic_slice_in_dim(route_weights, group_index * local_rows, local_rows, 0)
    expert_ids = jnp.arange(experts_total, dtype=jnp.int32)
    matched = (own_ids[:, :, None] == expert_ids[None, None, :]).astype(jnp.int32)
    flat_matched = matched.reshape(local_rows * top_k, experts_total)
    ranking = jnp.cumsum(flat_matched, axis=0) - 1
    slot_ids = jnp.arange(capacity, dtype=jnp.int32)
    hit = (flat_matched[:, :, None] == 1) & (ranking[:, :, None] == slot_ids[None, None, :])
    hit = hit.astype(jnp.int32).reshape(local_rows, top_k, experts_total, capacity)
    slot_weight = jnp.sum(hit.astype(jnp.float32) * own_gates[:, :, None, None], axis=1)
    slot_token = jnp.sum(hit, axis=1)
    token_ids = jnp.arange(local_rows, dtype=jnp.int32)
    slot_source = jnp.sum(slot_token * token_ids[:, None, None], axis=0)
    slot_used = jnp.sum(slot_token, axis=0) > 0

    slot_cols = jnp.where(slot_used[:, :, None], stream_cols[slot_source], 0.0).astype(jnp.bfloat16)
    slot_cols = jnp.broadcast_to(slot_cols[None], (groups,) + slot_cols.shape)
    slot_cols = slot_cols.reshape(groups * experts_total, capacity, columns)
    rows_in = spread_to_owners(slot_cols, ("dp", "expert"))
    rows_in = rows_in.reshape(groups, owners, capacity, columns).transpose(0, 2, 1, 3)
    stream_rows = rows_in.reshape(groups * capacity, model_width).astype(jnp.float32)
    inverse = lax.rsqrt(
        jnp.sum(stream_rows * stream_rows, axis=1, keepdims=True) / model_width + 1e-06
    )
    piece = (stream_rows * inverse).astype(jnp.bfloat16)
    gate_proj = jnp.dot(piece, w_gate[0], preferred_element_type=jnp.float32)
    up_proj = jnp.dot(piece, w_up[0], preferred_element_type=jnp.float32)
    hidden = (jax.nn.silu(gate_proj) * up_proj).astype(jnp.bfloat16)
    outputs = jnp.dot(hidden, w_down[0], preferred_element_type=jnp.float32)

    out_blocks = outputs.astype(jnp.bfloat16).reshape(groups, capacity, owners, columns)
    out_blocks = out_blocks.transpose(0, 2, 1, 3).reshape(groups * owners, capacity, columns)
    partials = spread_to_owners(out_blocks, ("dp", "expert"))
    partials = partials.reshape(groups, experts_total, capacity, columns)
    summed = jnp.sum(partials.astype(jnp.float32), axis=0)
    mix_cols = jnp.einsum(
        "tes,esc->tc", slot_weight, summed, precision=lax.Precision.HIGHEST
    ).astype(jnp.bfloat16)
    return (attn_cols, mix_cols)


def solution(mesh):
    in_specs = (
        P("dp", None),
        P("dp", None),
        P("dp", "expert", None),
        P("dp"),
        P(),
        P(),
        P(),
        P("expert", None),
        P("dp", None),
        P(),
        P(),
        P("expert", None, "dp"),
        P("expert", None, "dp"),
        P("expert", "dp", None),
    )
    out_specs = (P("dp", "expert"), P("dp", "expert"))
    return jax.shard_map(shards, mesh=mesh, in_specs=in_specs, out_specs=out_specs, check_vma=False)
```

```python
import math

import jax
import jax.numpy as jnp
from jax import lax
from jax.sharding import PartitionSpec as P

HD = 128
KVH = 4


def spread_to_owners(blocks, axis):
    return lax.all_to_all(blocks, axis, 0, 0, tiled=True)


def split_three(values):
    high = lax.reduce_precision(values, exponent_bits=8, mantissa_bits=7)
    rest = values - high
    middle = lax.reduce_precision(rest, exponent_bits=8, mantissa_bits=7)
    low = rest - middle
    return jnp.stack([high, middle, low]).astype(jnp.bfloat16)


def shards(
    query,
    new_kv,
    kv_cache,
    lengths,
    fork_parent,
    fork_child,
    fork_block,
    out_weight,
    residual,
    route_ids,
    route_weights,
    w_gate,
    w_up,
    w_down,
):
    groups = lax.axis_size("dp")
    owners = lax.axis_size("expert")
    group_index = lax.axis_index("dp")
    owner_index = lax.axis_index("expert")
    local_rows = query.shape[0]
    positions_dev = kv_cache.shape[1]
    key_width = KVH * HD
    head_count = query.shape[1] // HD
    grouping = head_count // KVH
    own_heads = head_count // owners
    model_width = residual.shape[1]
    columns = model_width // owners

    outgoing = (
        lax.dynamic_slice_in_dim(fork_parent, group_index * groups, groups)
        - group_index * local_rows
    )
    out_blocks = lax.dynamic_slice_in_dim(fork_block, group_index * groups, groups)
    send_rows = kv_cache[outgoing]
    arrived = lax.all_to_all(send_rows, "dp", split_axis=0, concat_axis=0, tiled=True)
    incoming = jnp.arange(groups, dtype=jnp.int32) * groups + group_index
    targets = fork_child[incoming] - group_index * local_rows
    take_new = owner_index >= fork_block[incoming]
    child_cache = jnp.where(take_new[:, None, None], arrived, kv_cache[targets])

    score_scale = 1.0 / math.sqrt(HD)
    positions = owner_index * positions_dev + jnp.arange(positions_dev, dtype=jnp.int32)

    def partial_attention(rows, cache_rows, row_lengths):
        count = rows.shape[0]
        visible = positions[None, :] < row_lengths[:, None]
        cached_keys = cache_rows[:, :, :key_width].reshape(count, positions_dev, KVH, HD)
        cached_values = cache_rows[:, :, key_width:].reshape(count, positions_dev, KVH, HD)
        grouped = rows.reshape(count, KVH, grouping, HD)
        scores = (
            jnp.einsum("bkgd,bpkd->bkgp", grouped, cached_keys, preferred_element_type=jnp.float32)
            * score_scale
        )
        scores = jnp.where(visible[:, None, None, :], scores, -1e30)
        highest = jnp.max(scores, axis=3)
        weights = jnp.where(visible[:, None, None, :], jnp.exp(scores - highest[..., None]), 0.0)
        weight_sum = jnp.sum(weights, axis=3)
        partial_out = jnp.einsum(
            "bkgp,bpkd->bkgd",
            weights.astype(jnp.bfloat16),
            cached_values,
            preferred_element_type=jnp.float32,
        )
        return partial_out, highest, weight_sum

    before_fork = partial_attention(query, kv_cache, lengths)
    of_children = partial_attention(query[targets], child_cache, lengths[targets])
    partial_out, highest, weight_sum = (
        whole.at[targets].set(child) for whole, child in zip(before_fork, of_children)
    )

    head_block = local_rows * own_heads
    send_out = partial_out.reshape(local_rows, owners, own_heads, HD).transpose(1, 0, 2, 3)
    send_peak = highest.reshape(local_rows, owners, own_heads).transpose(1, 0, 2)
    send_sum = weight_sum.reshape(local_rows, owners, own_heads).transpose(1, 0, 2)
    stats = jnp.stack([send_peak, send_sum], axis=1).reshape(owners, 2 * head_block)
    stat_parts = split_three(stats).transpose(1, 0, 2).reshape(owners, 6 * head_block)
    stat_width = -(-6 * head_block // HD) * HD
    stat_parts = jnp.pad(stat_parts, ((0, 0), (0, stat_width - 6 * head_block)))
    packed = jnp.concatenate(
        [
            send_out.astype(jnp.bfloat16).reshape(owners, head_block, HD),
            stat_parts.reshape(owners, stat_width // HD, HD),
        ],
        axis=1,
    )
    got = spread_to_owners(packed, "expert")
    got_out = got[:, :head_block].astype(jnp.float32).reshape(owners, local_rows, own_heads, HD)
    got_stats = got[:, head_block:].reshape(owners, stat_width)[:, : 6 * head_block]
    got_stats = got_stats.reshape(owners, 3, 2 * head_block).astype(jnp.float32)
    got_stats = (got_stats[:, 0] + got_stats[:, 1]) + got_stats[:, 2]
    got_stats = got_stats.reshape(owners, 2, local_rows, own_heads)
    got_peak = got_stats[:, 0]
    got_sum = got_stats[:, 1]
    head_peak = jnp.max(got_peak, axis=0)
    factors = jnp.exp(got_peak - head_peak[None])
    head_out = jnp.sum(got_out * factors[..., None], axis=0)
    head_sum = jnp.sum(got_sum * factors, axis=0)

    own_query = lax.dynamic_slice_in_dim(query, owner_index * own_heads * HD, own_heads * HD, 1)
    own_query = own_query.reshape(local_rows, own_heads, HD).astype(jnp.float32)
    kv_index = (owner_index * own_heads + jnp.arange(own_heads, dtype=jnp.int32)) // grouping
    new_keys = jnp.take(
        new_kv[:, :key_width].reshape(local_rows, KVH, HD), kv_index, axis=1
    ).astype(jnp.float32)
    new_values = jnp.take(
        new_kv[:, key_width:].reshape(local_rows, KVH, HD), kv_index, axis=1
    ).astype(jnp.float32)
    own_score = jnp.sum(own_query * new_keys, axis=2) * score_scale
    new_peak = jnp.maximum(head_peak, own_score)
    old_factor = jnp.exp(head_peak - new_peak)
    own_weight = jnp.exp(own_score - new_peak)
    denominator = head_sum * old_factor + own_weight
    own_rounded = lax.optimization_barrier(own_weight.astype(jnp.bfloat16)).astype(jnp.float32)
    attended = (
        head_out * old_factor[..., None] + own_rounded[..., None] * new_values
    ) / denominator[..., None]
    attended = attended.astype(jnp.bfloat16).reshape(local_rows, own_heads * HD)

    proj_blocks = jnp.einsum(
        "bd,doc->obc",
        attended,
        out_weight.reshape(own_heads * HD, owners, columns),
        preferred_element_type=jnp.float32,
    )
    got_proj = spread_to_owners(proj_blocks.astype(jnp.bfloat16), "expert")
    projected_cols = jnp.sum(got_proj.astype(jnp.float32), axis=0)
    attn_cols = projected_cols.astype(jnp.bfloat16)
    residual_cols = lax.dynamic_slice_in_dim(residual, owner_index * columns, columns, 1)
    stream_cols = residual_cols.astype(jnp.float32) + projected_cols

    top_k = route_ids.shape[1]
    experts_total = w_gate.shape[0] * owners
    capacity = max(2, 2 * local_rows * top_k // experts_total)
    own_ids = lax.dynamic_slice_in_dim(route_ids, group_index * local_rows, local_rows, 0)
    own_gates = lax.dynamic_slice_in_dim(route_weights, group_index * local_rows, local_rows, 0)
    expert_ids = jnp.arange(experts_total, dtype=jnp.int32)
    matched = (own_ids[:, :, None] == expert_ids[None, None, :]).astype(jnp.int32)
    flat_matched = matched.reshape(local_rows * top_k, experts_total)
    ranking = jnp.cumsum(flat_matched, axis=0) - 1
    slot_ids = jnp.arange(capacity, dtype=jnp.int32)
    hit = (flat_matched[:, :, None] == 1) & (ranking[:, :, None] == slot_ids[None, None, :])
    hit = hit.astype(jnp.int32).reshape(local_rows, top_k, experts_total, capacity)
    slot_weight = jnp.sum(hit.astype(jnp.float32) * own_gates[:, :, None, None], axis=1)
    slot_token = jnp.sum(hit, axis=1)
    token_ids = jnp.arange(local_rows, dtype=jnp.int32)
    slot_source = jnp.sum(slot_token * token_ids[:, None, None], axis=0)
    slot_used = jnp.sum(slot_token, axis=0) > 0

    slot_cols = jnp.where(slot_used[:, :, None], stream_cols[slot_source], 0.0).astype(jnp.bfloat16)
    slot_cols = jnp.broadcast_to(slot_cols[None], (groups,) + slot_cols.shape)
    slot_cols = slot_cols.reshape(groups * experts_total, capacity, columns)
    rows_in = spread_to_owners(slot_cols, ("dp", "expert"))
    rows_in = rows_in.reshape(groups, owners, capacity, columns).transpose(0, 2, 1, 3)
    stream_rows = rows_in.reshape(groups * capacity, model_width).astype(jnp.float32)
    inverse = lax.rsqrt(
        jnp.sum(stream_rows * stream_rows, axis=1, keepdims=True) / model_width + 1e-06
    )
    piece = (stream_rows * inverse).astype(jnp.bfloat16)
    gate_proj = jnp.dot(piece, w_gate[0], preferred_element_type=jnp.float32)
    up_proj = jnp.dot(piece, w_up[0], preferred_element_type=jnp.float32)
    hidden = (jax.nn.silu(gate_proj) * up_proj).astype(jnp.bfloat16)
    outputs = jnp.dot(hidden, w_down[0], preferred_element_type=jnp.float32)

    out_blocks = outputs.astype(jnp.bfloat16).reshape(groups, capacity, owners, columns)
    out_blocks = out_blocks.transpose(0, 2, 1, 3).reshape(groups * owners, capacity, columns)
    partials = spread_to_owners(out_blocks, ("dp", "expert"))
    partials = partials.reshape(groups, experts_total, capacity, columns)
    summed = jnp.sum(partials.astype(jnp.float32), axis=0)
    mix_cols = jnp.einsum(
        "tes,esc->tc", slot_weight, summed, precision=lax.Precision.HIGHEST
    ).astype(jnp.bfloat16)
    return (attn_cols, mix_cols)


def solution(mesh):
    in_specs = (
        P("dp", None),
        P("dp", None),
        P("dp", "expert", None),
        P("dp"),
        P(),
        P(),
        P(),
        P("expert", None),
        P("dp", None),
        P(),
        P(),
        P("expert", None, "dp"),
        P("expert", None, "dp"),
        P("expert", "dp", None),
    )
    out_specs = (P("dp", "expert"), P("dp", "expert"))
    return jax.shard_map(shards, mesh=mesh, in_specs=in_specs, out_specs=out_specs, check_vma=False)
```

```python
import math

import jax
import jax.numpy as jnp
from jax import lax
from jax.sharding import PartitionSpec as P

HD = 128
KVH = 4


def spread_to_owners(blocks, axis):
    return lax.all_to_all(blocks, axis, 0, 0, tiled=True)


def split_three(values):
    high = lax.reduce_precision(values, exponent_bits=8, mantissa_bits=7)
    rest = values - high
    middle = lax.reduce_precision(rest, exponent_bits=8, mantissa_bits=7)
    low = rest - middle
    return jnp.stack([high, middle, low]).astype(jnp.bfloat16)


def shards(
    query,
    new_kv,
    kv_cache,
    lengths,
    fork_parent,
    fork_child,
    fork_block,
    out_weight,
    residual,
    route_ids,
    route_weights,
    w_gate,
    w_up,
    w_down,
):
    groups = lax.axis_size("dp")
    owners = lax.axis_size("expert")
    group_index = lax.axis_index("dp")
    owner_index = lax.axis_index("expert")
    local_rows = query.shape[0]
    positions_dev = kv_cache.shape[1]
    key_width = KVH * HD
    head_count = query.shape[1] // HD
    grouping = head_count // KVH
    own_heads = head_count // owners
    model_width = residual.shape[1]
    columns = model_width // owners

    outgoing = (
        lax.dynamic_slice_in_dim(fork_parent, group_index * groups, groups)
        - group_index * local_rows
    )
    out_blocks = lax.dynamic_slice_in_dim(fork_block, group_index * groups, groups)
    send_rows = jnp.where(
        (owner_index >= out_blocks)[:, None, None],
        kv_cache[outgoing],
        jnp.zeros((), kv_cache.dtype),
    )
    arrived = lax.all_to_all(send_rows, "dp", split_axis=0, concat_axis=0, tiled=True)
    incoming = jnp.arange(groups, dtype=jnp.int32) * groups + group_index
    targets = fork_child[incoming] - group_index * local_rows
    take_new = owner_index >= fork_block[incoming]
    cache = kv_cache.at[targets].set(jnp.where(take_new[:, None, None], arrived, kv_cache[targets]))

    score_scale = 1.0 / math.sqrt(HD)
    positions = owner_index * positions_dev + jnp.arange(positions_dev, dtype=jnp.int32)
    visible = positions[None, :] < lengths[:, None]
    cached_keys = cache[:, :, :key_width].reshape(local_rows, positions_dev, KVH, HD)
    cached_values = cache[:, :, key_width:].reshape(local_rows, positions_dev, KVH, HD)
    grouped = query.reshape(local_rows, KVH, grouping, HD)
    scores = (
        jnp.einsum("bkgd,bpkd->bkgp", grouped, cached_keys, preferred_element_type=jnp.float32)
        * score_scale
    )
    scores = jnp.where(visible[:, None, None, :], scores, -1e30)
    highest = jnp.max(scores, axis=3)
    weights = jnp.where(visible[:, None, None, :], jnp.exp(scores - highest[..., None]), 0.0)
    weight_sum = jnp.sum(weights, axis=3)
    partial_out = jnp.einsum(
        "bkgp,bpkd->bkgd",
        weights.astype(jnp.bfloat16),
        cached_values,
        preferred_element_type=jnp.float32,
    )

    head_block = local_rows * own_heads
    send_out = partial_out.reshape(local_rows, owners, own_heads, HD).transpose(1, 0, 2, 3)
    send_peak = highest.reshape(local_rows, owners, own_heads).transpose(1, 0, 2)
    send_sum = weight_sum.reshape(local_rows, owners, own_heads).transpose(1, 0, 2)
    stats = jnp.stack([send_peak, send_sum], axis=1).reshape(owners, 2 * head_block)
    stat_parts = split_three(stats).transpose(1, 0, 2).reshape(owners, 6 * head_block)
    stat_width = -(-6 * head_block // HD) * HD
    stat_parts = jnp.pad(stat_parts, ((0, 0), (0, stat_width - 6 * head_block)))
    packed = jnp.concatenate(
        [
            send_out.astype(jnp.bfloat16).reshape(owners, head_block, HD),
            stat_parts.reshape(owners, stat_width // HD, HD),
        ],
        axis=1,
    )
    got = spread_to_owners(packed, "expert")
    got_out = got[:, :head_block].astype(jnp.float32).reshape(owners, local_rows, own_heads, HD)
    got_stats = got[:, head_block:].reshape(owners, stat_width)[:, : 6 * head_block]
    got_stats = got_stats.reshape(owners, 3, 2 * head_block).astype(jnp.float32)
    got_stats = (got_stats[:, 0] + got_stats[:, 1]) + got_stats[:, 2]
    got_stats = got_stats.reshape(owners, 2, local_rows, own_heads)
    got_peak = got_stats[:, 0]
    got_sum = got_stats[:, 1]
    head_peak = jnp.max(got_peak, axis=0)
    factors = jnp.exp(got_peak - head_peak[None])
    head_out = jnp.sum(got_out * factors[..., None], axis=0)
    head_sum = jnp.sum(got_sum * factors, axis=0)

    own_query = lax.dynamic_slice_in_dim(query, owner_index * own_heads * HD, own_heads * HD, 1)
    own_query = own_query.reshape(local_rows, own_heads, HD).astype(jnp.float32)
    kv_index = (owner_index * own_heads + jnp.arange(own_heads, dtype=jnp.int32)) // grouping
    new_keys = jnp.take(
        new_kv[:, :key_width].reshape(local_rows, KVH, HD), kv_index, axis=1
    ).astype(jnp.float32)
    new_values = jnp.take(
        new_kv[:, key_width:].reshape(local_rows, KVH, HD), kv_index, axis=1
    ).astype(jnp.float32)
    own_score = jnp.sum(own_query * new_keys, axis=2) * score_scale
    new_peak = jnp.maximum(head_peak, own_score)
    old_factor = jnp.exp(head_peak - new_peak)
    own_weight = jnp.exp(own_score - new_peak)
    denominator = head_sum * old_factor + own_weight
    own_rounded = lax.optimization_barrier(own_weight.astype(jnp.bfloat16)).astype(jnp.float32)
    attended = (
        head_out * old_factor[..., None] + own_rounded[..., None] * new_values
    ) / denominator[..., None]
    attended = attended.astype(jnp.bfloat16).reshape(local_rows, own_heads * HD)

    proj_blocks = jnp.einsum(
        "bd,doc->obc",
        attended,
        out_weight.reshape(own_heads * HD, owners, columns),
        preferred_element_type=jnp.float32,
    )
    got_proj = spread_to_owners(proj_blocks.astype(jnp.bfloat16), "expert")
    projected_cols = jnp.sum(got_proj.astype(jnp.float32), axis=0)
    attn_cols = projected_cols.astype(jnp.bfloat16)
    residual_cols = lax.dynamic_slice_in_dim(residual, owner_index * columns, columns, 1)
    stream_cols = residual_cols.astype(jnp.float32) + projected_cols

    top_k = route_ids.shape[1]
    experts_total = w_gate.shape[0] * owners
    capacity = max(2, 2 * local_rows * top_k // experts_total)
    own_ids = lax.dynamic_slice_in_dim(route_ids, group_index * local_rows, local_rows, 0)
    own_gates = lax.dynamic_slice_in_dim(route_weights, group_index * local_rows, local_rows, 0)
    expert_ids = jnp.arange(experts_total, dtype=jnp.int32)
    matched = (own_ids[:, :, None] == expert_ids[None, None, :]).astype(jnp.int32)
    flat_matched = matched.reshape(local_rows * top_k, experts_total)
    ranking = jnp.cumsum(flat_matched, axis=0) - 1
    slot_ids = jnp.arange(capacity, dtype=jnp.int32)
    hit = (flat_matched[:, :, None] == 1) & (ranking[:, :, None] == slot_ids[None, None, :])
    hit = hit.astype(jnp.int32).reshape(local_rows, top_k, experts_total, capacity)
    slot_weight = jnp.sum(hit.astype(jnp.float32) * own_gates[:, :, None, None], axis=1)
    slot_token = jnp.sum(hit, axis=1)
    token_ids = jnp.arange(local_rows, dtype=jnp.int32)
    slot_source = jnp.sum(slot_token * token_ids[:, None, None], axis=0)
    slot_used = jnp.sum(slot_token, axis=0) > 0

    slot_cols = jnp.where(slot_used[:, :, None], stream_cols[slot_source], 0.0).astype(jnp.bfloat16)
    slot_cols = jnp.broadcast_to(slot_cols[None], (groups,) + slot_cols.shape)
    slot_cols = slot_cols.reshape(groups * experts_total, capacity, columns)
    rows_in = spread_to_owners(slot_cols, ("dp", "expert"))
    rows_in = rows_in.reshape(groups, owners, capacity, columns).transpose(0, 2, 1, 3)
    stream_rows = rows_in.reshape(groups * capacity, model_width).astype(jnp.float32)
    inverse = lax.rsqrt(
        jnp.sum(stream_rows * stream_rows, axis=1, keepdims=True) / model_width + 1e-06
    )
    piece = (stream_rows * inverse).astype(jnp.bfloat16)
    gate_proj = jnp.dot(piece, w_gate[0], preferred_element_type=jnp.float32)
    up_proj = jnp.dot(piece, w_up[0], preferred_element_type=jnp.float32)
    hidden = (jax.nn.silu(gate_proj) * up_proj).astype(jnp.bfloat16)
    outputs = jnp.dot(hidden, w_down[0], preferred_element_type=jnp.float32)

    out_blocks = outputs.astype(jnp.bfloat16).reshape(groups, capacity, owners, columns)
    out_blocks = out_blocks.transpose(0, 2, 1, 3).reshape(groups * owners, capacity, columns)
    partials = spread_to_owners(out_blocks, ("dp", "expert"))
    partials = partials.reshape(groups * experts_total * capacity, columns)
    shard_weight = jnp.broadcast_to(
        slot_weight.astype(jnp.bfloat16)[:, None], (local_rows, groups) + slot_weight.shape[1:]
    ).reshape(local_rows, groups * experts_total * capacity)
    mix_cols = jnp.dot(shard_weight, partials, preferred_element_type=jnp.float32).astype(
        jnp.bfloat16
    )
    return (attn_cols, mix_cols)


def solution(mesh):
    in_specs = (
        P("dp", None),
        P("dp", None),
        P("dp", "expert", None),
        P("dp"),
        P(),
        P(),
        P(),
        P("expert", None),
        P("dp", None),
        P(),
        P(),
        P("expert", None, "dp"),
        P("expert", None, "dp"),
        P("expert", "dp", None),
    )
    out_specs = (P("dp", "expert"), P("dp", "expert"))
    return jax.shard_map(shards, mesh=mesh, in_specs=in_specs, out_specs=out_specs, check_vma=False)
```
